128 devices in a mesh: blk: 32 (over x, z_hi, y), rep: 4 (over z_lo, core).
Axes of the slice: x: 4, y: 4, z: 4 (z_hi: 2, z_lo: 2; z = z_hi * 2 + z_lo), core: 2. Of those that a mesh axis runs over, the one named last changes fastest.
Arguments:
- queries: bfloat16 [32768, 4096], P(('blk', 'rep')), as said below
- query_group: int32 [32768, 1], P(('blk', 'rep')), may hold values from 0 to 3; in each aligned block of 256 rows (0 to 255, 256 to 511, ...) at most 128 rows name the same one
- query_bin: int32 [32768], P(('blk', 'rep')), may hold values from 0 to 63
- query_shift: int32 [32768], P(('blk', 'rep')), may hold values from 1 to 2
- library: bfloat16 [4, 1024, 4096], P('rep', 'blk'), as said below
- library_bin: int32 [4, 1024], P('rep', 'blk'), may hold values from 0 to 63
Outputs:
- best_scores: float32 [32768, 8], P(('blk', 'rep'))
The draws below stay inside these ranges and needn't reach their ends.
Inputs may be any that keep to these rules, and one draw needn't show every extreme that they name: `query_group`: among the 256 queries of one device at most 128 name the same group, and on every draw some device has a group named by exactly 128 of its queries. `queries`: intensities are nonnegative and every spectrum has peaks. `library`: intensities are nonnegative and every spectrum has peaks.
All inputs are finite; a program needn't handle non-finite values.
Results may differ from the reference program's by a relative error of at most 0.0021.
Values may be sent and summed in bfloat16 or wider, within the bound.
No kernel may reach another device: no remote copies, remote signals or barrier semaphores. Data moves between devices by JAX's collectives and lax.ppermute only.
A program may use at most 192 MiB of HBM per device.

```python
import math
import jax
import jax.numpy as jnp
import numpy as np
from jax import lax

W = 4096
Q_DEV = 256
K = 8
NSHIFT = 2
SHIFT_BINS = 16
GBINS = 64
WIN = 16
GROUPS = 4
CAP = 128
QUERIES = 32768
LIB_G = 1024


def spectra(key, shape):
    k_one, k_two, k_three = jax.random.split(key, 3)
    present = jax.random.uniform(k_one, shape) < 0.3
    peak = jnp.exp(2.5 * jax.random.normal(k_two, shape, jnp.float32))
    scale = jnp.exp(jax.random.uniform(k_three, shape[:-1] + (1,), jnp.float32, 0.0, math.log(10.0)))
    first = jnp.zeros(shape, jnp.float32).at[..., 7].set(1.0)
    values = jnp.where(present, peak * scale, 0.0) + first * scale
    return values.astype(jnp.float32)


def draw_queries(key, part):
    return spectra(jax.random.fold_in(key, 11), (QUERIES, W)).astype(jnp.bfloat16)


def draw_library(key, part):
    return spectra(jax.random.fold_in(key, 23), (GROUPS, LIB_G, W)).astype(jnp.bfloat16)


def set_ends(array, key, low, high):
    longest = array.shape.index(max(array.shape))
    spots = []
    for shift in (0, 1):
        where = [jax.random.randint(jax.random.fold_in(key, axis), (), 0, length) for axis, length in enumerate(array.shape)]
        where[longest] = (where[longest] + shift) % array.shape[longest]
        spots.append(tuple(where))
    return array.at[spots[0]].set(low).at[spots[1]].set(high)


def routed_block(own_key, own, number, rows, count, top, bound, lean):
    ranking = jax.random.permutation(own_key, count)
    packed, common = shares(count, rows * top, bound, lean, True), shares(count, rows * top, bound, lean, False)
    places = jnp.arange(count)

    def named(tallies, turn):
        used = int((tallies > 0).sum())
        fixed = max(1, used // 4)
        moved = fixed + (places - fixed + turn * (used - fixed)) % max(1, count - fixed)
        return jnp.zeros((count,), jnp.int32).at[ranking[jnp.where(places < fixed, places, moved)]].set(jnp.asarray(tallies, jnp.int32))

    tallies = jnp.where(number % 4 == 0, named(packed, number // 4), named(common, number - number // 4 - 1))
    mixed = jax.random.permutation(jax.random.fold_in(own, 3), count)
    source_of, sink = mixed[0:count // 2 * 2:2], mixed[1:count // 2 * 2:2]
    room = jnp.minimum(tallies[source_of] - 1, bound - tallies[sink]) // 2
    room = jnp.where((source_of == ranking[0]) | (sink == ranking[0]) | (tallies[sink] == 0), 0, jnp.maximum(room, 0))
    moved = jax.random.randint(jax.random.fold_in(own, 4), (count // 2,), 0, 1 << 20) % (room + 1)
    tallies = tallies.at[source_of].add(-moved).at[sink].add(moved)
    items = jnp.searchsorted(jnp.cumsum(tallies), jnp.arange(rows * top), side="right").astype(jnp.int32)
    listing = items.reshape(top, rows).T
    listing = listing[jax.random.permutation(jax.random.fold_in(own, 1), rows)]
    turn = jax.random.randint(jax.random.fold_in(own, 2), (rows, 1), 0, top)
    return jnp.take_along_axis(listing, (jnp.arange(top)[None, :] + turn) % top, axis=1)


def shares(number_of, total, reach, lean, full):
    portions = [(1 << 20) // math.isqrt(standing ** lean) + 1 for standing in range(1, number_of + 1)]
    largest = reach if full else min(reach, max(-(-total // number_of), total * portions[0] // sum(portions)))
    least = 1 if total - largest >= number_of - 1 else 0
    holding, spare = [largest] + [least] * (number_of - 1), total - largest - least * (number_of - 1)
    while spare > 0:
        free = [i for i in range(1, number_of) if holding[i] < largest] or [i for i in range(1, number_of) if holding[i] < reach]
        pool, left = sum([portions[i] for i in free]), spare
        for i in free:
            extra = min(reach - holding[i], max(1, left * portions[i] // pool), spare)
            holding[i] = holding[i] + extra
            spare = spare - extra
    return np.array(holding)


def setup_inputs(seed: int = 0) -> dict:
    keys = jax.random.split(jax.random.key(seed), 7)
    queries = draw_queries(jax.random.fold_in(keys[6], 71), 0)
    query_group_keys = jax.random.split(jax.random.fold_in(keys[1], 1), QUERIES // Q_DEV)
    query_group_turns = jax.random.permutation(jax.random.fold_in(keys[1], 3), QUERIES // Q_DEV)
    query_group = jax.vmap(lambda own, number: routed_block(jax.random.fold_in(keys[1], 2), own, number, Q_DEV, GROUPS, 1, CAP, 2))(query_group_keys, query_group_turns).reshape((QUERIES, 1))
    query_bin = set_ends(jax.random.randint(keys[2], (QUERIES,), 0, GBINS), jax.random.fold_in(keys[2], 1), 0, GBINS - 1).astype(jnp.int32)
    query_shift = set_ends(jax.random.randint(keys[3], (QUERIES,), 1, NSHIFT + 1), jax.random.fold_in(keys[3], 1), 1, NSHIFT).astype(jnp.int32)
    library = draw_library(jax.random.fold_in(keys[6], 71), 0)
    library_bin = set_ends(jax.random.randint(keys[5], (GROUPS, LIB_G), 0, GBINS), jax.random.fold_in(keys[5], 1), 0, GBINS - 1).astype(jnp.int32)
    return {"queries": queries, "query_group": query_group, "query_bin": query_bin, "query_shift": query_shift, "library": library, "library_bin": library_bin}


def unit_rows(raw):
    values = jnp.sqrt(raw.astype(jnp.float32))
    total = lax.optimization_barrier(jnp.sum(values * values, axis=-1, keepdims=True))
    return (values * lax.rsqrt(total + 1e-06)).astype(jnp.bfloat16)

def lower_bins(rows, amount):
    tail = jnp.zeros(rows.shape[:-1] + (amount,), rows.dtype)
    return jnp.concatenate([rows[..., amount:], tail], axis=-1)

def slot_index(group, groups, capacity):
    labels = jnp.arange(groups, dtype=jnp.int32)
    onehot = (group[:, None] == labels[None, :]).astype(jnp.int32)
    before = jnp.cumsum(onehot, axis=0) - onehot
    place = lax.optimization_barrier(jnp.sum(before * onehot, axis=1)).astype(jnp.int32)
    return (group * capacity + place).astype(jnp.int32)

def slot_source(slot, count, slots):
    start = jnp.full((slots,), count, jnp.int32)
    return start.at[slot].set(jnp.arange(count, dtype=jnp.int32))

def reference(queries, query_group, query_bin, query_shift, library, library_bin):
    blocks = QUERIES // Q_DEV
    slots = GROUPS * CAP
    unit_q = unit_rows(queries).reshape(blocks, Q_DEV, W)
    group = query_group[:, 0].reshape(blocks, Q_DEV)
    bins = query_bin.reshape(blocks, Q_DEV)
    shifts = query_shift.reshape(blocks, Q_DEV)
    slot = jax.vmap(lambda g: slot_index(g, GROUPS, CAP))(group)
    source = jax.vmap(lambda s: slot_source(s, Q_DEV, slots))(slot)
    pad_q = jnp.concatenate([unit_q, jnp.zeros((blocks, 1, W), unit_q.dtype)], axis=1)
    pad_bin = jnp.concatenate([bins, jnp.zeros((blocks, 1), jnp.int32)], axis=1)
    pad_shift = jnp.concatenate([shifts, jnp.zeros((blocks, 1), jnp.int32)], axis=1)
    take = jax.vmap(lambda a, i: a[i])
    slot_q = take(pad_q, source).reshape(blocks, GROUPS, CAP, W)
    slot_bin = take(pad_bin, source).reshape(blocks, GROUPS, CAP)
    slot_shift = take(pad_shift, source).reshape(blocks, GROUPS, CAP)
    unit_lib = unit_rows(library)
    results = []
    for g in range(GROUPS):
        lib_f = unit_lib[g].astype(jnp.float32)
        lib_bin = library_bin[g]

        def per_block(item):
            rows, qbin, qshift = item
            moved = jnp.zeros_like(rows)
            for s in range(1, NSHIFT + 1):
                moved = jnp.where((qshift == s)[:, None], lower_bins(rows, s * SHIFT_BINS), moved)
            both = jnp.concatenate([rows, moved], axis=0).astype(jnp.float32)
            prod = jnp.dot(lib_f, both.T, preferred_element_type=jnp.float32)
            plain = prod[:, :CAP]
            shifted = prod[:, CAP:]
            near = jnp.abs(lib_bin[:, None] - qbin[None, :]) <= WIN
            score = jnp.where(near, jnp.maximum(plain, shifted), 0.0)
            return lax.top_k(score.T, K)[0]
        results.append(lax.map(per_block, (slot_q[:, g], slot_bin[:, g], slot_shift[:, g])))
    stacked = jnp.stack(results, axis=1).reshape(blocks, slots, K)
    best = take(stacked, slot)
    return best.reshape(QUERIES, K)
```

```python
import jax
import jax.numpy as jnp
from jax import lax
from jax.sharding import Mesh
from jax.sharding import PartitionSpec as P

W = 4096
K = 8
NSHIFT = 2
SHIFT_BINS = 16
WIN = 16
CAP = 128
BLK = ("blk_0", "blk_1", "blk_2")
BLK_REP = ("blk_0", "blk_1", "blk_2", "rep")
ZRING = ("blk_1", "rep")


def ring_index(z, core):
    return (z // 2) * 4 + (z % 2) * 2 + core


UP = [(ring_index(z, 0), ring_index((z + 1) % 4, 0)) for z in range(4)] + [
    (ring_index(z, 1), ring_index((z + 3) % 4, 1)) for z in range(4)
]
CROSS = [(ring_index(z, 1), ring_index((z + 1) % 4, 0)) for z in range(4)] + [
    (ring_index(z, 0), ring_index((z + 3) % 4, 1)) for z in range(4)
]
SIBLING = [(ring_index(z, c), ring_index(z, 1 - c)) for z in range(4) for c in range(2)]


def inverse(perm):
    return [(b, a) for a, b in perm]


def unit_rows(raw):
    values = jnp.sqrt(raw.astype(jnp.float32))
    total = jnp.sum(values * values, axis=-1, keepdims=True)
    return (values * lax.rsqrt(total + 1e-06)).astype(jnp.bfloat16)


def lower_bins(rows, amount):
    tail = jnp.zeros(rows.shape[:-1] + (amount,), rows.dtype)
    return jnp.concatenate([rows[..., amount:], tail], axis=-1)


def slot_index(role, roles, capacity):
    labels = jnp.arange(roles, dtype=jnp.int32)
    onehot = (role[:, None] == labels[None, :]).astype(jnp.int32)
    before = jnp.cumsum(onehot, axis=0) - onehot
    place = jnp.sum(before * onehot, axis=1)
    return role * capacity + place


def top_rows(scores):
    height = scores.shape[0]
    position = lax.broadcasted_iota(jnp.int32, scores.shape, 0)
    picked = []
    for step in range(K):
        top = jnp.max(scores, axis=0)
        first = jnp.min(jnp.where(scores == top[None, :], position, height), axis=0)
        picked.append(top)
        scores = jnp.where(position == first[None, :], -3e38, scores)
    return jnp.stack(picked, axis=1)


def route(blocks, perms):
    return [blocks[0]] + [lax.ppermute(b, ZRING, p) for b, p in zip(blocks[1:], perms)]


def on_device(queries, query_group, query_bin, query_shift, library, library_bin):
    lib_rows = library.shape[1]
    z_lo = lax.axis_index("rep") // 2
    core = lax.axis_index("rep") % 2
    roles = 4
    slots = roles * CAP

    unit_lib = unit_rows(library[0])
    bin_row = jnp.pad(library_bin.astype(jnp.bfloat16), ((0, 0), (0, W - lib_rows)))
    packed_lib = jnp.concatenate([unit_lib, bin_row], axis=0)
    half = lax.all_gather(packed_lib, "blk_1", axis=0, tiled=True)
    full = lax.all_gather(half, ("blk_0", "blk_2"), axis=0, tiled=True)
    stride = lib_rows + 1
    blocks_n = full.shape[0] // stride
    lib_bins = full.reshape(blocks_n, stride, W)[:, lib_rows, :stride].reshape(-1)
    lib_bins = lib_bins.astype(jnp.int32)
    valid = (jnp.arange(full.shape[0], dtype=jnp.int32) % stride) != lib_rows

    unit_q = unit_rows(queries)
    group = query_group[:, 0]
    role = ((group // 2) != z_lo).astype(jnp.int32) * 2 + ((group % 2) != core).astype(jnp.int32)
    slot = slot_index(role, roles, CAP)
    slot_ids = jnp.arange(slots, dtype=jnp.int32)
    placed = slot[:, None] == slot_ids[None, :]
    placed_int = placed.astype(jnp.int32)
    send_q = lax.dot_general(
        placed.astype(jnp.bfloat16), unit_q, (((0,), (0,)), ((), ())),
        preferred_element_type=jnp.float32,
    ).astype(jnp.bfloat16).reshape(roles, CAP, W)
    send_bin = jnp.sum(placed_int * query_bin[:, None], axis=0).reshape(roles, CAP)
    send_shift = jnp.sum(placed_int * query_shift[:, None], axis=0).reshape(roles, CAP)
    send_meta = jnp.stack([send_bin, send_shift], axis=1)

    perms = (SIBLING, UP, CROSS)
    rows = jnp.concatenate(route([send_q[i] for i in range(roles)], perms), axis=0)
    meta = jnp.stack(route([send_meta[i] for i in range(roles)], perms), axis=0)
    flat_bin = meta[:, 0].reshape(-1)
    flat_shift = meta[:, 1].reshape(-1)
    total = rows.shape[0]

    moved = jnp.zeros_like(rows)
    for s in range(1, NSHIFT + 1):
        moved = jnp.where((flat_shift == s)[:, None], lower_bins(rows, s * SHIFT_BINS), moved)
    both = jnp.concatenate([rows, moved], axis=0)
    prod = lax.dot_general(full, both, (((1,), (1,)), ((), ())), preferred_element_type=jnp.float32)
    near = (jnp.abs(lib_bins[:, None] - flat_bin[None, :]) <= WIN) & valid[:, None]
    scores = jnp.where(near, jnp.maximum(prod[:, :total], prod[:, total:]), 0.0)
    scores = jnp.where(valid[:, None], scores, -1.0)
    best = top_rows(scores).reshape(roles, CAP, K)

    home = route([best[i] for i in range(roles)], tuple(inverse(p) for p in perms))
    home = jnp.concatenate(home, axis=0)
    return jnp.take(home, slot, axis=0)


def solution(mesh):
    split = Mesh(
        mesh.devices.reshape(4, 2, 4, mesh.shape["rep"]), ("blk_0", "blk_1", "blk_2", "rep")
    )
    in_specs = (
        P(BLK_REP, None),
        P(BLK_REP, None),
        P(BLK_REP),
        P(BLK_REP),
        P("rep", BLK, None),
        P("rep", BLK),
    )
    out_specs = P(BLK_REP, None)
    return jax.shard_map(
        on_device, mesh=split, in_specs=in_specs, out_specs=out_specs, check_vma=False
    )
```

```python
import jax
import jax.numpy as jnp
from jax import lax
from jax.sharding import Mesh
from jax.sharding import PartitionSpec as P

W = 4096
K = 8
NSHIFT = 2
SHIFT_BINS = 16
WIN = 16
CAP = 128
BLK = ("blk_0", "blk_1", "blk_2")
BLK_REP = ("blk_0", "blk_1", "blk_2", "rep")
ZRING = ("blk_1", "rep")


def ring_index(z, core):
    return (z // 2) * 4 + (z % 2) * 2 + core


UP = [(ring_index(z, 0), ring_index((z + 1) % 4, 0)) for z in range(4)] + [
    (ring_index(z, 1), ring_index((z + 3) % 4, 1)) for z in range(4)
]
CROSS = [(ring_index(z, 1), ring_index((z + 1) % 4, 0)) for z in range(4)] + [
    (ring_index(z, 0), ring_index((z + 3) % 4, 1)) for z in range(4)
]
SIBLING = [(ring_index(z, c), ring_index(z, 1 - c)) for z in range(4) for c in range(2)]


def inverse(perm):
    return [(b, a) for a, b in perm]


def unit_rows(raw):
    values = jnp.sqrt(raw.astype(jnp.float32))
    total = jnp.sum(values * values, axis=-1, keepdims=True)
    return (values * lax.rsqrt(total + 1e-06)).astype(jnp.bfloat16)


def lower_bins(rows, amount):
    tail = jnp.zeros(rows.shape[:-1] + (amount,), rows.dtype)
    return jnp.concatenate([rows[..., amount:], tail], axis=-1)


def slot_index(role, roles, capacity):
    labels = jnp.arange(roles, dtype=jnp.int32)
    onehot = (role[:, None] == labels[None, :]).astype(jnp.int32)
    before = jnp.cumsum(onehot, axis=0) - onehot
    place = jnp.sum(before * onehot, axis=1)
    return role * capacity + place


SORT8 = (
    ((0, 1), (2, 3), (4, 5), (6, 7)),
    ((0, 2), (1, 3), (4, 6), (5, 7)),
    ((1, 2), (5, 6)),
    ((0, 4), (1, 5), (2, 6), (3, 7)),
    ((2, 4), (3, 5)),
    ((1, 2), (3, 4), (5, 6)),
)


def exchange(lists, i, j):
    lists[i], lists[j] = jnp.maximum(lists[i], lists[j]), jnp.minimum(lists[i], lists[j])


def top_rows(scores):
    depth = scores.shape[0] // K
    lists = [scores[k * depth:(k + 1) * depth] for k in range(K)]
    for stage in SORT8:
        for i, j in stage:
            exchange(lists, i, j)
    while depth > 1:
        depth //= 2
        lists = [jnp.maximum(lists[i][:depth], lists[K - 1 - i][depth:]) for i in range(K)]
        for step in (4, 2, 1):
            for i in range(K):
                if (i // step) % 2 == 0:
                    exchange(lists, i, i + step)
    return jnp.concatenate(lists, axis=0).T


def route(blocks, perms):
    return [blocks[0]] + [lax.ppermute(b, ZRING, p) for b, p in zip(blocks[1:], perms)]


def on_device(queries, query_group, query_bin, query_shift, library, library_bin):
    lib_rows = library.shape[1]
    z_lo = lax.axis_index("rep") // 2
    core = lax.axis_index("rep") % 2
    roles = 4
    slots = roles * CAP

    z_hi = lax.axis_index("blk_1")
    unit_lib = unit_rows(library[0])
    partner = lax.ppermute(unit_lib, "blk_1", [(0, 1), (1, 0)])
    pair = jnp.where(z_hi == 0, jnp.concatenate([unit_lib, partner], axis=0),
                     jnp.concatenate([partner, unit_lib], axis=0))
    full = lax.all_gather(pair, ("blk_0", "blk_2"), axis=0, tiled=True)
    lib_bins = lax.all_gather(library_bin[0], ("blk_0", "blk_2", "blk_1"), axis=0, tiled=True)

    unit_q = unit_rows(queries)
    group = query_group[:, 0]
    role = ((group // 2) != z_lo).astype(jnp.int32) * 2 + ((group % 2) != core).astype(jnp.int32)
    slot = slot_index(role, roles, CAP)
    slot_ids = jnp.arange(slots, dtype=jnp.int32)
    placed = slot[:, None] == slot_ids[None, :]
    placed_int = placed.astype(jnp.int32)
    send_q = lax.dot_general(
        placed.astype(jnp.bfloat16), unit_q, (((0,), (0,)), ((), ())),
        preferred_element_type=jnp.float32,
    ).astype(jnp.bfloat16).reshape(roles, CAP, W)
    send_bin = jnp.sum(placed_int * query_bin[:, None], axis=0).reshape(roles, CAP)
    send_shift = jnp.sum(placed_int * query_shift[:, None], axis=0).reshape(roles, CAP)
    send_meta = jnp.stack([send_bin, send_shift], axis=1)

    perms = (SIBLING, UP, CROSS)
    rows = jnp.concatenate(route([send_q[i] for i in range(roles)], perms), axis=0)
    meta = jnp.stack(route([send_meta[i] for i in range(roles)], perms), axis=0)
    flat_bin = meta[:, 0].reshape(-1)
    flat_shift = meta[:, 1].reshape(-1)
    total = rows.shape[0]

    moved = jnp.zeros_like(rows)
    for s in range(1, NSHIFT + 1):
        moved = jnp.where((flat_shift == s)[:, None], lower_bins(rows, s * SHIFT_BINS), moved)
    both = jnp.concatenate([rows, moved], axis=0)
    prod = lax.dot_general(full, both, (((1,), (1,)), ((), ())), preferred_element_type=jnp.float32)
    near = jnp.abs(lib_bins[:, None] - flat_bin[None, :]) <= WIN
    scores = jnp.where(near, jnp.maximum(prod[:, :total], prod[:, total:]), 0.0)
    best = top_rows(scores).reshape(roles, CAP, K)

    home = route([best[i] for i in range(roles)], tuple(inverse(p) for p in perms))
    home = jnp.concatenate(home, axis=0)
    return jnp.take(home, slot, axis=0)


def solution(mesh):
    split = Mesh(
        mesh.devices.reshape(4, 2, 4, mesh.shape["rep"]), ("blk_0", "blk_1", "blk_2", "rep")
    )
    in_specs = (
        P(BLK_REP, None),
        P(BLK_REP, None),
        P(BLK_REP),
        P(BLK_REP),
        P("rep", BLK, None),
        P("rep", BLK),
    )
    out_specs = P(BLK_REP, None)
    return jax.shard_map(
        on_device, mesh=split, in_specs=in_specs, out_specs=out_specs, check_vma=False
    )
```

```python
import jax
import jax.numpy as jnp
from jax import lax
from jax.sharding import Mesh
from jax.sharding import PartitionSpec as P

W = 4096
K = 8
NSHIFT = 2
SHIFT_BINS = 16
WIN = 16
CAP = 128
LANE = 128
BLK = ("blk_0", "blk_1", "blk_2")
BLK_REP = ("blk_0", "blk_1", "blk_2", "rep")
ZRING = ("blk_1", "rep")


def ring_index(z, core):
    return (z // 2) * 4 + (z % 2) * 2 + core


UP = [(ring_index(z, 0), ring_index((z + 1) % 4, 0)) for z in range(4)] + [
    (ring_index(z, 1), ring_index((z + 3) % 4, 1)) for z in range(4)
]
CROSS = [(ring_index(z, 1), ring_index((z + 1) % 4, 0)) for z in range(4)] + [
    (ring_index(z, 0), ring_index((z + 3) % 4, 1)) for z in range(4)
]
SIBLING = [(ring_index(z, c), ring_index(z, 1 - c)) for z in range(4) for c in range(2)]


def inverse(perm):
    return [(b, a) for a, b in perm]


def unit_rows(raw):
    values = jnp.sqrt(raw.astype(jnp.float32))
    total = jnp.sum(values * values, axis=-1, keepdims=True)
    return (values * lax.rsqrt(total + 1e-06)).astype(jnp.bfloat16)


def lower_bins(rows, amount):
    tail = jnp.zeros(rows.shape[:-1] + (amount,), rows.dtype)
    return jnp.concatenate([rows[..., amount:], tail], axis=-1)


def slot_index(role, roles, capacity):
    labels = jnp.arange(roles, dtype=jnp.int32)
    onehot = (role[:, None] == labels[None, :]).astype(jnp.int32)
    before = jnp.cumsum(onehot, axis=0) - onehot
    place = jnp.sum(before * onehot, axis=1)
    return role * capacity + place


SORT8 = (
    ((0, 1), (2, 3), (4, 5), (6, 7)),
    ((0, 2), (1, 3), (4, 6), (5, 7)),
    ((1, 2), (5, 6)),
    ((0, 4), (1, 5), (2, 6), (3, 7)),
    ((2, 4), (3, 5)),
    ((1, 2), (3, 4), (5, 6)),
)


def exchange(lists, i, j):
    lists[i], lists[j] = jnp.maximum(lists[i], lists[j]), jnp.minimum(lists[i], lists[j])


def bitonic_merge(first, second, depth):
    lists = [jnp.maximum(first[i][:depth], second[K - 1 - i][:depth]) for i in range(K)]
    for step in (4, 2, 1):
        for i in range(K):
            if (i // step) % 2 == 0:
                exchange(lists, i, i + step)
    return lists


def top_rows(scores):
    depth = scores.shape[0] // K
    lists = [scores[k * depth:(k + 1) * depth] for k in range(K)]
    for stage in SORT8:
        for i, j in stage:
            exchange(lists, i, j)
    while depth > 1:
        depth //= 2
        lists = bitonic_merge(lists, [a[depth:] for a in lists], depth)
    return lists


def route(blocks, perms):
    return [blocks[0]] + [lax.ppermute(b, ZRING, p) for b, p in zip(blocks[1:], perms)]


def on_device(queries, query_group, query_bin, query_shift, library, library_bin):
    z_lo = lax.axis_index("rep") // 2
    core = lax.axis_index("rep") % 2
    roles = 4
    slots = roles * CAP

    unit_lib = unit_rows(library[0])
    bin_cols = jnp.pad(library_bin[0].astype(jnp.bfloat16)[:, None], ((0, 0), (0, LANE - 1)))
    packed = jnp.concatenate([unit_lib, bin_cols], axis=1)
    partner = lax.ppermute(packed, "blk_1", [(0, 1), (1, 0)])
    near_lib = lax.all_gather(packed, ("blk_0", "blk_2"), axis=0, tiled=True)
    far_lib = lax.all_gather(partner, ("blk_0", "blk_2"), axis=0, tiled=True)

    unit_q = unit_rows(queries)
    group = query_group[:, 0]
    role = ((group // 2) != z_lo).astype(jnp.int32) * 2 + ((group % 2) != core).astype(jnp.int32)
    slot = slot_index(role, roles, CAP)
    slot_ids = jnp.arange(slots, dtype=jnp.int32)
    placed = slot[:, None] == slot_ids[None, :]
    placed_int = placed.astype(jnp.int32)
    send_q = lax.dot_general(
        placed.astype(jnp.bfloat16), unit_q, (((0,), (0,)), ((), ())),
        preferred_element_type=jnp.float32,
    ).astype(jnp.bfloat16).reshape(roles, CAP, W)
    send_bin = jnp.sum(placed_int * query_bin[:, None], axis=0).reshape(roles, CAP)
    send_shift = jnp.sum(placed_int * query_shift[:, None], axis=0).reshape(roles, CAP)
    send_meta = jnp.stack([send_bin, send_shift], axis=1)

    perms = (SIBLING, UP, CROSS)
    rows = jnp.concatenate(route([send_q[i] for i in range(roles)], perms), axis=0)
    meta = jnp.stack(route([send_meta[i] for i in range(roles)], perms), axis=0)
    flat_bin = meta[:, 0].reshape(-1)
    flat_shift = meta[:, 1].reshape(-1)
    total = rows.shape[0]

    moved = jnp.zeros_like(rows)
    for s in range(1, NSHIFT + 1):
        moved = jnp.where((flat_shift == s)[:, None], lower_bins(rows, s * SHIFT_BINS), moved)
    both = jnp.pad(jnp.concatenate([rows, moved], axis=0), ((0, 0), (0, LANE)))

    def best_of(lib):
        prod = lax.dot_general(lib, both, (((1,), (1,)), ((), ())), preferred_element_type=jnp.float32)
        lib_bins = lib[:, W].astype(jnp.int32)
        near = jnp.abs(lib_bins[:, None] - flat_bin[None, :]) <= WIN
        return top_rows(jnp.where(near, jnp.maximum(prod[:, :total], prod[:, total:]), 0.0))

    best = bitonic_merge(best_of(near_lib), best_of(far_lib), 1)
    best = jnp.concatenate(best, axis=0).T.reshape(roles, CAP, K)

    home = route([best[i] for i in range(roles)], tuple(inverse(p) for p in perms))
    home = jnp.concatenate(home, axis=0)
    return jnp.take(home, slot, axis=0)


def solution(mesh):
    split = Mesh(
        mesh.devices.reshape(4, 2, 4, mesh.shape["rep"]), ("blk_0", "blk_1", "blk_2", "rep")
    )
    in_specs = (
        P(BLK_REP, None),
        P(BLK_REP, None),
        P(BLK_REP),
        P(BLK_REP),
        P("rep", BLK, None),
        P("rep", BLK),
    )
    out_specs = P(BLK_REP, None)
    return jax.shard_map(
        on_device, mesh=split, in_specs=in_specs, out_specs=out_specs, check_vma=False
    )
```

```python
import jax
import jax.numpy as jnp
from jax import lax
from jax.sharding import Mesh
from jax.sharding import PartitionSpec as P

W = 4096
K = 8
NSHIFT = 2
SHIFT_BINS = 16
WIN = 16
CAP = 128
LANE = 128
BLK = ("blk_0", "blk_1", "blk_2")
BLK_REP = ("blk_0", "blk_1", "blk_2", "rep")
ZRING = ("blk_1", "rep")


def ring_index(z, core):
    return (z // 2) * 4 + (z % 2) * 2 + core


UP = [(ring_index(z, 0), ring_index((z + 1) % 4, 0)) for z in range(4)] + [
    (ring_index(z, 1), ring_index((z + 3) % 4, 1)) for z in range(4)
]
CROSS = [(ring_index(z, 1), ring_index((z + 1) % 4, 0)) for z in range(4)] + [
    (ring_index(z, 0), ring_index((z + 3) % 4, 1)) for z in range(4)
]
SIBLING = [(ring_index(z, c), ring_index(z, 1 - c)) for z in range(4) for c in range(2)]


def inverse(perm):
    return [(b, a) for a, b in perm]


def unit_rows(raw):
    values = jnp.sqrt(raw.astype(jnp.float32))
    total = jnp.sum(values * values, axis=-1, keepdims=True)
    return (values * lax.rsqrt(total + 1e-06)).astype(jnp.bfloat16)


def lower_bins(rows, amount):
    tail = jnp.zeros(rows.shape[:-1] + (amount,), rows.dtype)
    return jnp.concatenate([rows[..., amount:], tail], axis=-1)


def slot_index(role, roles, capacity):
    labels = jnp.arange(roles, dtype=jnp.int32)
    onehot = (role[:, None] == labels[None, :]).astype(jnp.int32)
    before = jnp.cumsum(onehot, axis=0) - onehot
    place = jnp.sum(before * onehot, axis=1)
    return role * capacity + place


SORT8 = (
    ((0, 1), (2, 3), (4, 5), (6, 7)),
    ((0, 2), (1, 3), (4, 6), (5, 7)),
    ((1, 2), (5, 6)),
    ((0, 4), (1, 5), (2, 6), (3, 7)),
    ((2, 4), (3, 5)),
    ((1, 2), (3, 4), (5, 6)),
)


def exchange(lists, i, j):
    lists[i], lists[j] = jnp.maximum(lists[i], lists[j]), jnp.minimum(lists[i], lists[j])


def bitonic_merge(first, second, depth):
    lists = [jnp.maximum(first[i][:depth], second[K - 1 - i][:depth]) for i in range(K)]
    for step in (4, 2, 1):
        for i in range(K):
            if (i // step) % 2 == 0:
                exchange(lists, i, i + step)
    return lists


def top_rows(scores):
    depth = scores.shape[0] // K
    lists = [scores[k * depth:(k + 1) * depth] for k in range(K)]
    for stage in SORT8:
        for i, j in stage:
            exchange(lists, i, j)
    while depth > 1:
        depth //= 2
        lists = bitonic_merge(lists, [a[depth:] for a in lists], depth)
    return lists


def ring_gather(block, axis):
    size = 4
    up = [(i, (i + 1) % size) for i in range(size)]
    down = [(i, (i - 1) % size) for i in range(size)]
    below = lax.ppermute(block, axis, up)
    above = lax.ppermute(block, axis, down)
    half = block.shape[0] // 2
    far_low = lax.ppermute(below[:half], axis, up)
    far_high = lax.ppermute(above[half:], axis, down)
    return [block, below, above, far_low, far_high]


def route(blocks, perms):
    return [blocks[0]] + [lax.ppermute(b, ZRING, p) for b, p in zip(blocks[1:], perms)]


def on_device(queries, query_group, query_bin, query_shift, library, library_bin):
    z_lo = lax.axis_index("rep") // 2
    core = lax.axis_index("rep") % 2
    roles = 4
    slots = roles * CAP

    unit_lib = unit_rows(library[0])
    bin_cols = jnp.pad(library_bin[0].astype(jnp.bfloat16)[:, None], ((0, 0), (0, LANE - 1)))
    packed = jnp.concatenate([unit_lib, bin_cols], axis=1)
    partner = lax.ppermute(packed, "blk_1", [(0, 1), (1, 0)])
    chunk = jnp.concatenate([packed, partner], axis=0)
    half = chunk.shape[0] // 2
    x_first = ring_gather(chunk[:half], "blk_0")
    y_first = ring_gather(chunk[half:], "blk_2")
    x_then_y = ring_gather(jnp.concatenate(x_first, axis=0), "blk_2")
    y_then_x = ring_gather(jnp.concatenate(y_first, axis=0), "blk_0")
    early = jnp.concatenate([chunk] + x_first[1:] + y_first[1:], axis=0)
    middle = jnp.concatenate(x_then_y[1:3] + y_then_x[1:3], axis=0)
    late = jnp.concatenate(x_then_y[3:] + y_then_x[3:], axis=0)

    unit_q = unit_rows(queries)
    group = query_group[:, 0]
    role = ((group // 2) != z_lo).astype(jnp.int32) * 2 + ((group % 2) != core).astype(jnp.int32)
    slot = slot_index(role, roles, CAP)
    slot_ids = jnp.arange(slots, dtype=jnp.int32)
    placed = slot[:, None] == slot_ids[None, :]
    placed_int = placed.astype(jnp.int32)
    send_q = lax.dot_general(
        placed.astype(jnp.bfloat16), unit_q, (((0,), (0,)), ((), ())),
        preferred_element_type=jnp.float32,
    ).astype(jnp.bfloat16).reshape(roles, CAP, W)
    send_bin = jnp.sum(placed_int * query_bin[:, None], axis=0).reshape(roles, CAP)
    send_shift = jnp.sum(placed_int * query_shift[:, None], axis=0).reshape(roles, CAP)
    send_meta = jnp.stack([send_bin, send_shift], axis=1)

    perms = (SIBLING, UP, CROSS)
    rows = jnp.concatenate(route([send_q[i] for i in range(roles)], perms), axis=0)
    meta = jnp.stack(route([send_meta[i] for i in range(roles)], perms), axis=0)
    flat_bin = meta[:, 0].reshape(-1)
    flat_shift = meta[:, 1].reshape(-1)
    total = rows.shape[0]

    moved = jnp.zeros_like(rows)
    for s in range(1, NSHIFT + 1):
        moved = jnp.where((flat_shift == s)[:, None], lower_bins(rows, s * SHIFT_BINS), moved)
    both = jnp.pad(jnp.concatenate([rows, moved], axis=0), ((0, 0), (0, LANE)))

    def best_of(lib):
        prod = lax.dot_general(lib, both, (((1,), (1,)), ((), ())), preferred_element_type=jnp.float32)
        lib_bins = lib[:, W].astype(jnp.int32)
        near = jnp.abs(lib_bins[:, None] - flat_bin[None, :]) <= WIN
        return top_rows(jnp.where(near, jnp.maximum(prod[:, :total], prod[:, total:]), 0.0))

    best = bitonic_merge(best_of(early), best_of(middle), 1)
    best = bitonic_merge(best, best_of(late), 1)
    best = jnp.concatenate(best, axis=0).T.reshape(roles, CAP, K)

    home = route([best[i] for i in range(roles)], tuple(inverse(p) for p in perms))
    home = jnp.concatenate(home, axis=0)
    return jnp.take(home, slot, axis=0)


def solution(mesh):
    split = Mesh(
        mesh.devices.reshape(4, 2, 4, mesh.shape["rep"]), ("blk_0", "blk_1", "blk_2", "rep")
    )
    in_specs = (
        P(BLK_REP, None),
        P(BLK_REP, None),
        P(BLK_REP),
        P(BLK_REP),
        P("rep", BLK, None),
        P("rep", BLK),
    )
    out_specs = P(BLK_REP, None)
    return jax.shard_map(
        on_device, mesh=split, in_specs=in_specs, out_specs=out_specs, check_vma=False
    )
```

```python
import jax
import jax.numpy as jnp
from jax import lax
from jax.sharding import Mesh
from jax.sharding import PartitionSpec as P

W = 4096
K = 8
NSHIFT = 2
SHIFT_BINS = 16
WIN = 16
CAP = 128
LANE = 128
BLK = ("blk_0", "blk_1", "blk_2")
BLK_REP = ("blk_0", "blk_1", "blk_2", "rep")
ZRING = ("blk_1", "rep")


def ring_index(z, core):
    return (z // 2) * 4 + (z % 2) * 2 + core


UP = [(ring_index(z, 0), ring_index((z + 1) % 4, 0)) for z in range(4)] + [
    (ring_index(z, 1), ring_index((z + 3) % 4, 1)) for z in range(4)
]
CROSS = [(ring_index(z, 1), ring_index((z + 1) % 4, 0)) for z in range(4)] + [
    (ring_index(z, 0), ring_index((z + 3) % 4, 1)) for z in range(4)
]
SIBLING = [(ring_index(z, c), ring_index(z, 1 - c)) for z in range(4) for c in range(2)]


def inverse(perm):
    return [(b, a) for a, b in perm]


def unit_rows(raw):
    values = jnp.sqrt(raw.astype(jnp.float32))
    total = jnp.sum(values * values, axis=-1, keepdims=True)
    return (values * lax.rsqrt(total + 1e-06)).astype(jnp.bfloat16)


def lower_bins(rows, amount):
    tail = jnp.zeros(rows.shape[:-1] + (amount,), rows.dtype)
    return jnp.concatenate([rows[..., amount:], tail], axis=-1)


def slot_index(role, roles, capacity):
    labels = jnp.arange(roles, dtype=jnp.int32)
    onehot = (role[:, None] == labels[None, :]).astype(jnp.int32)
    before = jnp.cumsum(onehot, axis=0) - onehot
    place = jnp.sum(before * onehot, axis=1)
    return role * capacity + place


SORT8 = (
    ((0, 1), (2, 3), (4, 5), (6, 7)),
    ((0, 2), (1, 3), (4, 6), (5, 7)),
    ((1, 2), (5, 6)),
    ((0, 4), (1, 5), (2, 6), (3, 7)),
    ((2, 4), (3, 5)),
    ((1, 2), (3, 4), (5, 6)),
)


def exchange(lists, i, j):
    lists[i], lists[j] = jnp.maximum(lists[i], lists[j]), jnp.minimum(lists[i], lists[j])


def bitonic_merge(first, second, depth):
    lists = [jnp.maximum(first[i][:depth], second[K - 1 - i][:depth]) for i in range(K)]
    for step in (4, 2, 1):
        for i in range(K):
            if (i // step) % 2 == 0:
                exchange(lists, i, i + step)
    return lists


def top_rows(scores):
    depth = scores.shape[0] // K
    assert depth & (depth - 1) == 0
    lists = [scores[k * depth:(k + 1) * depth] for k in range(K)]
    for stage in SORT8:
        for i, j in stage:
            exchange(lists, i, j)
    while depth > 1:
        depth //= 2
        lists = bitonic_merge(lists, [a[depth:] for a in lists], depth)
    return lists


def ring_gather(block, axis):
    size = 4
    up = [(i, (i + 1) % size) for i in range(size)]
    down = [(i, (i - 1) % size) for i in range(size)]
    below = lax.ppermute(block, axis, up)
    above = lax.ppermute(block, axis, down)
    half = block.shape[0] // 2
    far_low = lax.ppermute(below[:half], axis, up)
    far_high = lax.ppermute(above[half:], axis, down)
    return [block, below, above, far_low, far_high]


def route(blocks, perms):
    return [blocks[0]] + [lax.ppermute(b, ZRING, p) for b, p in zip(blocks[1:], perms)]


def on_device(queries, query_group, query_bin, query_shift, library, library_bin):
    z_lo = lax.axis_index("rep") // 2
    core = lax.axis_index("rep") % 2
    roles = 4
    slots = roles * CAP

    unit_lib = unit_rows(library[0])
    bin_cols = jnp.pad(library_bin[0].astype(jnp.bfloat16)[:, None], ((0, 0), (0, LANE - 1)))
    packed = jnp.concatenate([unit_lib, bin_cols], axis=1)
    partner = lax.ppermute(packed, "blk_1", [(0, 1), (1, 0)])
    chunk = jnp.concatenate([packed, partner], axis=0)
    half = chunk.shape[0] // 2
    gathered = lax.all_gather(chunk[:half], ("blk_0", "blk_2"), axis=0, tiled=True)
    y_first = ring_gather(chunk[half:], "blk_2")
    y_then_x = ring_gather(jnp.concatenate(y_first, axis=0), "blk_0")
    middle = jnp.concatenate(y_then_x[1:3], axis=0)
    late = jnp.concatenate(y_then_x[3:], axis=0)

    unit_q = unit_rows(queries)
    group = query_group[:, 0]
    role = ((group // 2) != z_lo).astype(jnp.int32) * 2 + ((group % 2) != core).astype(jnp.int32)
    slot = slot_index(role, roles, CAP)
    slot_ids = jnp.arange(slots, dtype=jnp.int32)
    placed = slot[:, None] == slot_ids[None, :]
    placed_int = placed.astype(jnp.int32)
    send_q = lax.dot_general(
        placed.astype(jnp.bfloat16), unit_q, (((0,), (0,)), ((), ())),
        preferred_element_type=jnp.float32,
    ).astype(jnp.bfloat16).reshape(roles, CAP, W)
    send_bin = jnp.sum(placed_int * query_bin[:, None], axis=0).reshape(roles, CAP)
    send_shift = jnp.sum(placed_int * query_shift[:, None], axis=0).reshape(roles, CAP)
    send_meta = jnp.stack([send_bin, send_shift], axis=1)

    perms = (SIBLING, UP, CROSS)
    rows = jnp.concatenate(route([send_q[i] for i in range(roles)], perms), axis=0)
    meta = jnp.stack(route([send_meta[i] for i in range(roles)], perms), axis=0)
    flat_bin = meta[:, 0].reshape(-1)
    flat_shift = meta[:, 1].reshape(-1)
    total = rows.shape[0]

    moved = jnp.zeros_like(rows)
    for s in range(1, NSHIFT + 1):
        moved = jnp.where((flat_shift == s)[:, None], lower_bins(rows, s * SHIFT_BINS), moved)
    both = jnp.pad(jnp.concatenate([rows, moved], axis=0), ((0, 0), (0, LANE)))

    def best_of(lib):
        prod = lax.dot_general(lib, both, (((1,), (1,)), ((), ())), preferred_element_type=jnp.float32)
        lib_bins = lib[:, W].astype(jnp.int32)
        near = jnp.abs(lib_bins[:, None] - flat_bin[None, :]) <= WIN
        return top_rows(jnp.where(near, jnp.maximum(prod[:, :total], prod[:, total:]), 0.0))

    best = bitonic_merge(best_of(y_then_x[0]), best_of(middle), 1)
    best = bitonic_merge(best, best_of(late), 1)
    best = bitonic_merge(best, best_of(gathered), 1)
    best = jnp.concatenate(best, axis=0).T.reshape(roles, CAP, K)

    home = route([best[i] for i in range(roles)], tuple(inverse(p) for p in perms))
    home = jnp.concatenate(home, axis=0)
    return jnp.take(home, slot, axis=0)


def solution(mesh):
    split = Mesh(
        mesh.devices.reshape(4, 2, 4, mesh.shape["rep"]), ("blk_0", "blk_1", "blk_2", "rep")
    )
    in_specs = (
        P(BLK_REP, None),
        P(BLK_REP, None),
        P(BLK_REP),
        P(BLK_REP),
        P("rep", BLK, None),
        P("rep", BLK),
    )
    out_specs = P(BLK_REP, None)
    return jax.shard_map(
        on_device, mesh=split, in_specs=in_specs, out_specs=out_specs, check_vma=False
    )
```

```python
import jax
import jax.numpy as jnp
from jax import lax
from jax.sharding import Mesh
from jax.sharding import PartitionSpec as P

W = 4096
K = 8
NSHIFT = 2
SHIFT_BINS = 16
WIN = 16
CAP = 128
LANE = 128
BLK = ("blk_0", "blk_1", "blk_2")
BLK_REP = ("blk_0", "blk_1", "blk_2", "rep")
ZRING = ("blk_1", "rep")


def ring_index(z, core):
    return (z // 2) * 4 + (z % 2) * 2 + core


UP = [(ring_index(z, 0), ring_index((z + 1) % 4, 0)) for z in range(4)] + [
    (ring_index(z, 1), ring_index((z + 3) % 4, 1)) for z in range(4)
]
CROSS = [(ring_index(z, 1), ring_index((z + 1) % 4, 0)) for z in range(4)] + [
    (ring_index(z, 0), ring_index((z + 3) % 4, 1)) for z in range(4)
]
SIBLING = [(ring_index(z, c), ring_index(z, 1 - c)) for z in range(4) for c in range(2)]


def inverse(perm):
    return [(b, a) for a, b in perm]


def unit_rows(raw):
    values = jnp.sqrt(raw.astype(jnp.float32))
    total = jnp.sum(values * values, axis=-1, keepdims=True)
    return (values * lax.rsqrt(total + 1e-06)).astype(jnp.bfloat16)


def lower_bins(rows, amount):
    tail = jnp.zeros(rows.shape[:-1] + (amount,), rows.dtype)
    return jnp.concatenate([rows[..., amount:], tail], axis=-1)


def slot_index(role, roles, capacity):
    labels = jnp.arange(roles, dtype=jnp.int32)
    onehot = (role[:, None] == labels[None, :]).astype(jnp.int32)
    before = jnp.cumsum(onehot, axis=0) - onehot
    place = jnp.sum(before * onehot, axis=1)
    return role * capacity + place


SORT8 = (
    ((0, 1), (2, 3), (4, 5), (6, 7)),
    ((0, 2), (1, 3), (4, 6), (5, 7)),
    ((1, 2), (5, 6)),
    ((0, 4), (1, 5), (2, 6), (3, 7)),
    ((2, 4), (3, 5)),
    ((1, 2), (3, 4), (5, 6)),
)


def exchange(lists, i, j):
    lists[i], lists[j] = jnp.maximum(lists[i], lists[j]), jnp.minimum(lists[i], lists[j])


def bitonic_merge(first, second, depth):
    lists = [jnp.maximum(first[i][:depth], second[K - 1 - i][:depth]) for i in range(K)]
    for step in (4, 2, 1):
        for i in range(K):
            if (i // step) % 2 == 0:
                exchange(lists, i, i + step)
    return lists


def top_rows(scores):
    depth = scores.shape[0] // K
    assert depth & (depth - 1) == 0
    lists = [scores[k * depth:(k + 1) * depth] for k in range(K)]
    for stage in SORT8:
        for i, j in stage:
            exchange(lists, i, j)
    while depth > 1:
        depth //= 2
        lists = bitonic_merge(lists, [a[depth:] for a in lists], depth)
    return lists


def ring_gather(block, axis):
    size = 4
    up = [(i, (i + 1) % size) for i in range(size)]
    down = [(i, (i - 1) % size) for i in range(size)]
    below = lax.ppermute(block, axis, up)
    above = lax.ppermute(block, axis, down)
    half = block.shape[0] // 2
    far_low = lax.ppermute(below[:half], axis, up)
    far_high = lax.ppermute(above[half:], axis, down)
    return [block, below, above, far_low, far_high]


def route(blocks, perms):
    return [blocks[0]] + [lax.ppermute(b, ZRING, p) for b, p in zip(blocks[1:], perms)]


def on_device(queries, query_group, query_bin, query_shift, library, library_bin):
    z_lo = lax.axis_index("rep") // 2
    core = lax.axis_index("rep") % 2
    roles = 4
    slots = roles * CAP

    unit_lib = unit_rows(library[0])
    bin_cols = jnp.pad(library_bin[0].astype(jnp.bfloat16)[:, None], ((0, 0), (0, LANE - 1)))
    packed = jnp.concatenate([unit_lib, bin_cols], axis=1)
    partner = lax.ppermute(packed, "blk_1", [(0, 1), (1, 0)])
    chunk = jnp.concatenate([packed, partner], axis=0)
    gathered = lax.all_gather(chunk, ("blk_0", "blk_2"), axis=0, tiled=True)

    unit_q = unit_rows(queries)
    group = query_group[:, 0]
    role = ((group // 2) != z_lo).astype(jnp.int32) * 2 + ((group % 2) != core).astype(jnp.int32)
    slot = slot_index(role, roles, CAP)
    slot_ids = jnp.arange(slots, dtype=jnp.int32)
    placed = slot[:, None] == slot_ids[None, :]
    placed_int = placed.astype(jnp.int32)
    send_q = lax.dot_general(
        placed.astype(jnp.bfloat16), unit_q, (((0,), (0,)), ((), ())),
        preferred_element_type=jnp.float32,
    ).astype(jnp.bfloat16).reshape(roles, CAP, W)
    send_bin = jnp.sum(placed_int * query_bin[:, None], axis=0).reshape(roles, CAP)
    send_shift = jnp.sum(placed_int * query_shift[:, None], axis=0).reshape(roles, CAP)
    send_meta = jnp.stack([send_bin, send_shift], axis=1)

    perms = (SIBLING, UP, CROSS)
    rows = jnp.concatenate(route([send_q[i] for i in range(roles)], perms), axis=0)
    meta = jnp.stack(route([send_meta[i] for i in range(roles)], perms), axis=0)
    flat_bin = meta[:, 0].reshape(-1)
    flat_shift = meta[:, 1].reshape(-1)
    total = rows.shape[0]

    moved = jnp.zeros_like(rows)
    for s in range(1, NSHIFT + 1):
        moved = jnp.where((flat_shift == s)[:, None], lower_bins(rows, s * SHIFT_BINS), moved)
    both = jnp.pad(jnp.concatenate([rows, moved], axis=0), ((0, 0), (0, LANE)))

    def best_of(lib):
        prod = lax.dot_general(lib, both, (((1,), (1,)), ((), ())), preferred_element_type=jnp.float32)
        lib_bins = lib[:, W].astype(jnp.int32)
        near = jnp.abs(lib_bins[:, None] - flat_bin[None, :]) <= WIN
        return top_rows(jnp.where(near, jnp.maximum(prod[:, :total], prod[:, total:]), 0.0))

    best = best_of(gathered)
    best = jnp.concatenate(best, axis=0).T.reshape(roles, CAP, K)

    home = route([best[i] for i in range(roles)], tuple(inverse(p) for p in perms))
    home = jnp.concatenate(home, axis=0)
    return jnp.take(home, slot, axis=0)


def solution(mesh):
    split = Mesh(
        mesh.devices.reshape(4, 2, 4, mesh.shape["rep"]), ("blk_0", "blk_1", "blk_2", "rep")
    )
    in_specs = (
        P(BLK_REP, None),
        P(BLK_REP, None),
        P(BLK_REP),
        P(BLK_REP),
        P("rep", BLK, None),
        P("rep", BLK),
    )
    out_specs = P(BLK_REP, None)
    return jax.shard_map(
        on_device, mesh=split, in_specs=in_specs, out_specs=out_specs, check_vma=False
    )
```

```python
import jax
import jax.numpy as jnp
from jax import lax
from jax.sharding import Mesh
from jax.sharding import PartitionSpec as P

W = 4096
K = 8
NSHIFT = 2
SHIFT_BINS = 16
WIN = 16
CAP = 128
BLK = ("blk_0", "blk_1", "blk_2")
BLK_REP = ("blk_0", "blk_1", "blk_2", "rep")
ZRING = ("blk_1", "rep")


def ring_index(z, core):
    return (z // 2) * 4 + (z % 2) * 2 + core


UP = [(ring_index(z, 0), ring_index((z + 1) % 4, 0)) for z in range(4)] + [
    (ring_index(z, 1), ring_index((z + 3) % 4, 1)) for z in range(4)
]
CROSS = [(ring_index(z, 1), ring_index((z + 1) % 4, 0)) for z in range(4)] + [
    (ring_index(z, 0), ring_index((z + 3) % 4, 1)) for z in range(4)
]
SIBLING = [(ring_index(z, c), ring_index(z, 1 - c)) for z in range(4) for c in range(2)]


def inverse(perm):
    return [(b, a) for a, b in perm]


def unit_rows(raw):
    values = jnp.sqrt(raw.astype(jnp.float32))
    total = jnp.sum(values * values, axis=-1, keepdims=True)
    return (values * lax.rsqrt(total + 1e-06)).astype(jnp.bfloat16)


def lower_bins(rows, amount):
    tail = jnp.zeros(rows.shape[:-1] + (amount,), rows.dtype)
    return jnp.concatenate([rows[..., amount:], tail], axis=-1)


def slot_index(role, roles, capacity):
    labels = jnp.arange(roles, dtype=jnp.int32)
    onehot = (role[:, None] == labels[None, :]).astype(jnp.int32)
    before = jnp.cumsum(onehot, axis=0) - onehot
    place = jnp.sum(before * onehot, axis=1)
    return role * capacity + place


SORT8 = (
    ((0, 1), (2, 3), (4, 5), (6, 7)),
    ((0, 2), (1, 3), (4, 6), (5, 7)),
    ((1, 2), (5, 6)),
    ((0, 4), (1, 5), (2, 6), (3, 7)),
    ((2, 4), (3, 5)),
    ((1, 2), (3, 4), (5, 6)),
)


def exchange(lists, i, j):
    lists[i], lists[j] = jnp.maximum(lists[i], lists[j]), jnp.minimum(lists[i], lists[j])


def top_rows(scores):
    depth = scores.shape[0] // K
    lists = [scores[k * depth:(k + 1) * depth] for k in range(K)]
    for stage in SORT8:
        for i, j in stage:
            exchange(lists, i, j)
    while depth > 1:
        depth //= 2
        lists = [jnp.maximum(lists[i][:depth], lists[K - 1 - i][depth:]) for i in range(K)]
        for step in (4, 2, 1):
            for i in range(K):
                if (i // step) % 2 == 0:
                    exchange(lists, i, i + step)
    return jnp.concatenate(lists, axis=0).T


def route(blocks, perms):
    return [blocks[0]] + [lax.ppermute(b, ZRING, p) for b, p in zip(blocks[1:], perms)]


def on_device(queries, query_group, query_bin, query_shift, library, library_bin):
    lib_rows = library.shape[1]
    z_lo = lax.axis_index("rep") // 2
    core = lax.axis_index("rep") % 2
    roles = 4
    slots = roles * CAP

    partner = lax.ppermute(library[0], "blk_1", [(0, 1), (1, 0)])
    partner_bin = lax.ppermute(library_bin[0], "blk_1", [(0, 1), (1, 0)])
    chunk = jnp.concatenate([unit_rows(library[0]), unit_rows(partner)], axis=0)
    chunk_bin = jnp.concatenate([library_bin[0], partner_bin], axis=0)
    full, lib_bins = lax.all_gather((chunk, chunk_bin), ("blk_0", "blk_2"), axis=0, tiled=True)

    unit_q = unit_rows(queries)
    group = query_group[:, 0]
    role = ((group // 2) != z_lo).astype(jnp.int32) * 2 + ((group % 2) != core).astype(jnp.int32)
    slot = slot_index(role, roles, CAP)
    slot_ids = jnp.arange(slots, dtype=jnp.int32)
    placed = slot[:, None] == slot_ids[None, :]
    placed_int = placed.astype(jnp.int32)
    send_q = lax.dot_general(
        placed.astype(jnp.bfloat16), unit_q, (((0,), (0,)), ((), ())),
        preferred_element_type=jnp.float32,
    ).astype(jnp.bfloat16).reshape(roles, CAP, W)
    send_bin = jnp.sum(placed_int * query_bin[:, None], axis=0).reshape(roles, CAP)
    send_shift = jnp.sum(placed_int * query_shift[:, None], axis=0).reshape(roles, CAP)
    send_meta = jnp.stack([send_bin, send_shift], axis=1)

    perms = (SIBLING, UP, CROSS)
    rows = jnp.concatenate(route([send_q[i] for i in range(roles)], perms), axis=0)
    meta = jnp.stack(route([send_meta[i] for i in range(roles)], perms), axis=0)
    flat_bin = meta[:, 0].reshape(-1)
    flat_shift = meta[:, 1].reshape(-1)
    total = rows.shape[0]

    moved = jnp.zeros_like(rows)
    for s in range(1, NSHIFT + 1):
        moved = jnp.where((flat_shift == s)[:, None], lower_bins(rows, s * SHIFT_BINS), moved)
    both = jnp.concatenate([rows, moved], axis=0)
    prod = lax.dot_general(full, both, (((1,), (1,)), ((), ())), preferred_element_type=jnp.float32)
    near = jnp.abs(lib_bins[:, None] - flat_bin[None, :]) <= WIN
    scores = jnp.where(near, jnp.maximum(prod[:, :total], prod[:, total:]), 0.0)
    best = top_rows(scores).reshape(roles, CAP, K)

    home = route([best[i] for i in range(roles)], tuple(inverse(p) for p in perms))
    home = jnp.concatenate(home, axis=0)
    return jnp.take(home, slot, axis=0)


def solution(mesh):
    split = Mesh(
        mesh.devices.reshape(4, 2, 4, mesh.shape["rep"]), ("blk_0", "blk_1", "blk_2", "rep")
    )
    in_specs = (
        P(BLK_REP, None),
        P(BLK_REP, None),
        P(BLK_REP),
        P(BLK_REP),
        P("rep", BLK, None),
        P("rep", BLK),
    )
    out_specs = P(BLK_REP, None)
    return jax.shard_map(
        on_device, mesh=split, in_specs=in_specs, out_specs=out_specs, check_vma=False
    )
```

```python
import jax
import jax.numpy as jnp
from jax import lax
from jax.sharding import Mesh
from jax.sharding import PartitionSpec as P

W = 4096
K = 8
NSHIFT = 2
SHIFT_BINS = 16
WIN = 16
CAP = 128
LANE = 128
BLK = ("blk_0", "blk_1", "blk_2")
BLK_REP = ("blk_0", "blk_1", "blk_2", "rep")
ZRING = ("blk_1", "rep")


def ring_index(z, core):
    return (z // 2) * 4 + (z % 2) * 2 + core


UP = [(ring_index(z, 0), ring_index((z + 1) % 4, 0)) for z in range(4)] + [
    (ring_index(z, 1), ring_index((z + 3) % 4, 1)) for z in range(4)
]
CROSS = [(ring_index(z, 1), ring_index((z + 1) % 4, 0)) for z in range(4)] + [
    (ring_index(z, 0), ring_index((z + 3) % 4, 1)) for z in range(4)
]
SIBLING = [(ring_index(z, c), ring_index(z, 1 - c)) for z in range(4) for c in range(2)]


def inverse(perm):
    return [(b, a) for a, b in perm]


def unit_rows(raw):
    values = jnp.sqrt(raw.astype(jnp.float32))
    total = jnp.sum(values * values, axis=-1, keepdims=True)
    return (values * lax.rsqrt(total + 1e-06)).astype(jnp.bfloat16)


def lower_bins(rows, amount):
    tail = jnp.zeros(rows.shape[:-1] + (amount,), rows.dtype)
    return jnp.concatenate([rows[..., amount:], tail], axis=-1)


def slot_index(role, roles, capacity):
    labels = jnp.arange(roles, dtype=jnp.int32)
    onehot = (role[:, None] == labels[None, :]).astype(jnp.int32)
    before = jnp.cumsum(onehot, axis=0) - onehot
    place = jnp.sum(before * onehot, axis=1)
    return role * capacity + place


SORT8 = (
    ((0, 1), (2, 3), (4, 5), (6, 7)),
    ((0, 2), (1, 3), (4, 6), (5, 7)),
    ((1, 2), (5, 6)),
    ((0, 4), (1, 5), (2, 6), (3, 7)),
    ((2, 4), (3, 5)),
    ((1, 2), (3, 4), (5, 6)),
)


def exchange(lists, i, j):
    lists[i], lists[j] = jnp.maximum(lists[i], lists[j]), jnp.minimum(lists[i], lists[j])


def bitonic_merge(first, second, depth):
    lists = [jnp.maximum(first[i][:depth], second[K - 1 - i][:depth]) for i in range(K)]
    for step in (4, 2, 1):
        for i in range(K):
            if (i // step) % 2 == 0:
                exchange(lists, i, i + step)
    return lists


def top_rows(scores):
    depth = scores.shape[0] // K
    lists = [scores[k * depth:(k + 1) * depth] for k in range(K)]
    for stage in SORT8:
        for i, j in stage:
            exchange(lists, i, j)
    while depth > 1:
        depth //= 2
        lists = bitonic_merge(lists, [a[depth:] for a in lists], depth)
    return lists


def ring_gather(block, axis):
    size = 4
    up = [(i, (i + 1) % size) for i in range(size)]
    down = [(i, (i - 1) % size) for i in range(size)]
    below = lax.ppermute(block, axis, up)
    above = lax.ppermute(block, axis, down)
    half = block.shape[0] // 2
    far_low = lax.ppermute(below[:half], axis, up)
    far_high = lax.ppermute(above[half:], axis, down)
    return [block, below, above, far_low, far_high]


def route(blocks, perms):
    return [blocks[0]] + [lax.ppermute(b, ZRING, p) for b, p in zip(blocks[1:], perms)]


def on_device(queries, query_group, query_bin, query_shift, library, library_bin):
    z_lo = lax.axis_index("rep") // 2
    core = lax.axis_index("rep") % 2
    roles = 4
    slots = roles * CAP

    bin_cols = jnp.pad(library_bin[0].astype(jnp.bfloat16)[:, None], ((0, 0), (0, LANE - 1)))
    partner = lax.ppermute(jnp.concatenate([library[0], bin_cols], axis=1), "blk_1", [(0, 1), (1, 0)])
    own = jnp.concatenate([unit_rows(library[0]), bin_cols], axis=1)
    partner = jnp.concatenate([unit_rows(partner[:, :W]), partner[:, W:]], axis=1)
    half = own.shape[0]
    x_first = ring_gather(own, "blk_0")
    y_first = ring_gather(partner, "blk_2")

    unit_q = unit_rows(queries)
    meta_cols = jnp.stack([query_bin, query_shift], axis=1).astype(jnp.bfloat16)
    unit_q = jnp.concatenate([unit_q, jnp.pad(meta_cols, ((0, 0), (0, LANE - 2)))], axis=1)
    group = query_group[:, 0]
    role = ((group // 2) != z_lo).astype(jnp.int32) * 2 + ((group % 2) != core).astype(jnp.int32)
    slot = slot_index(role, roles, CAP)
    slot_ids = jnp.arange(slots, dtype=jnp.int32)
    placed = slot[:, None] == slot_ids[None, :]
    send_q = lax.dot_general(
        placed.astype(jnp.bfloat16), unit_q, (((0,), (0,)), ((), ())),
        preferred_element_type=jnp.float32,
    ).astype(jnp.bfloat16).reshape(roles, CAP, W + LANE)

    perms = (SIBLING, UP, CROSS)
    received = jnp.concatenate(route([send_q[i] for i in range(roles)], perms), axis=0)
    x_block, y_block, received = lax.optimization_barrier(
        (jnp.concatenate(x_first, axis=0), jnp.concatenate(y_first, axis=0), received))
    x_then_y = ring_gather(x_block, "blk_2")
    y_then_x = ring_gather(y_block, "blk_0")
    early = jnp.concatenate([own, partner] + x_first[1:] + y_first[1:], axis=0)
    middle = jnp.concatenate(x_then_y[1:3] + y_then_x[1:3], axis=0)
    late = jnp.concatenate(x_then_y[3:] + y_then_x[3:], axis=0)

    rows = received[:, :W]
    flat_bin = received[:, W].astype(jnp.int32)
    flat_shift = received[:, W + 1].astype(jnp.int32)
    total = rows.shape[0]

    moved = jnp.zeros_like(rows)
    for s in range(1, NSHIFT + 1):
        moved = jnp.where((flat_shift == s)[:, None], lower_bins(rows, s * SHIFT_BINS), moved)
    both = jnp.pad(jnp.concatenate([rows, moved], axis=0), ((0, 0), (0, LANE)))

    def best_of(lib):
        prod = lax.dot_general(lib, both, (((1,), (1,)), ((), ())), preferred_element_type=jnp.float32)
        lib_bins = lib[:, W].astype(jnp.int32)
        near = jnp.abs(lib_bins[:, None] - flat_bin[None, :]) <= WIN
        return top_rows(jnp.where(near, jnp.maximum(prod[:, :total], prod[:, total:]), 0.0))

    best = bitonic_merge(best_of(early), best_of(middle), 1)
    best = bitonic_merge(best, best_of(late), 1)
    best = jnp.concatenate(best, axis=0).T.reshape(roles, CAP, K)

    home = route([best[i] for i in range(roles)], tuple(inverse(p) for p in perms))
    home = jnp.concatenate(home, axis=0)
    return jnp.take(home, slot, axis=0)


def solution(mesh):
    split = Mesh(
        mesh.devices.reshape(4, 2, 4, mesh.shape["rep"]), ("blk_0", "blk_1", "blk_2", "rep")
    )
    in_specs = (
        P(BLK_REP, None),
        P(BLK_REP, None),
        P(BLK_REP),
        P(BLK_REP),
        P("rep", BLK, None),
        P("rep", BLK),
    )
    out_specs = P(BLK_REP, None)
    return jax.shard_map(
        on_device, mesh=split, in_specs=in_specs, out_specs=out_specs, check_vma=False
    )
```

```python
import jax
import jax.numpy as jnp
from jax import lax
from jax.sharding import Mesh
from jax.sharding import PartitionSpec as P

W = 4096
K = 8
NSHIFT = 2
SHIFT_BINS = 16
WIN = 16
CAP = 128
LANE = 128
BLK = ("blk_0", "blk_1", "blk_2")
BLK_REP = ("blk_0", "blk_1", "blk_2", "rep")
ZRING = ("blk_1", "rep")


def ring_index(z, core):
    return (z // 2) * 4 + (z % 2) * 2 + core


UP = [(ring_index(z, 0), ring_index((z + 1) % 4, 0)) for z in range(4)] + [
    (ring_index(z, 1), ring_index((z + 3) % 4, 1)) for z in range(4)
]
CROSS = [(ring_index(z, 1), ring_index((z + 1) % 4, 0)) for z in range(4)] + [
    (ring_index(z, 0), ring_index((z + 3) % 4, 1)) for z in range(4)
]
SIBLING = [(ring_index(z, c), ring_index(z, 1 - c)) for z in range(4) for c in range(2)]


def inverse(perm):
    return [(b, a) for a, b in perm]


def unit_rows(raw):
    values = jnp.sqrt(raw.astype(jnp.float32))
    total = jnp.sum(values * values, axis=-1, keepdims=True)
    return (values * lax.rsqrt(total + 1e-06)).astype(jnp.bfloat16)


def lower_bins(rows, amount):
    tail = jnp.zeros(rows.shape[:-1] + (amount,), rows.dtype)
    return jnp.concatenate([rows[..., amount:], tail], axis=-1)


def slot_index(role, roles, capacity):
    labels = jnp.arange(roles, dtype=jnp.int32)
    onehot = (role[:, None] == labels[None, :]).astype(jnp.int32)
    before = jnp.cumsum(onehot, axis=0) - onehot
    place = jnp.sum(before * onehot, axis=1)
    return role * capacity + place


SORT8 = (
    ((0, 1), (2, 3), (4, 5), (6, 7)),
    ((0, 2), (1, 3), (4, 6), (5, 7)),
    ((1, 2), (5, 6)),
    ((0, 4), (1, 5), (2, 6), (3, 7)),
    ((2, 4), (3, 5)),
    ((1, 2), (3, 4), (5, 6)),
)


def exchange(lists, i, j):
    lists[i], lists[j] = jnp.maximum(lists[i], lists[j]), jnp.minimum(lists[i], lists[j])


def bitonic_merge(first, second, depth):
    lists = [jnp.maximum(first[i][:depth], second[K - 1 - i][:depth]) for i in range(K)]
    for step in (4, 2, 1):
        for i in range(K):
            if (i // step) % 2 == 0:
                exchange(lists, i, i + step)
    return lists


def top_rows(scores):
    depth = scores.shape[0] // K
    lists = [scores[k * depth:(k + 1) * depth] for k in range(K)]
    for stage in SORT8:
        for i, j in stage:
            exchange(lists, i, j)
    while depth > 1:
        depth //= 2
        lists = bitonic_merge(lists, [a[depth:] for a in lists], depth)
    return lists


def ring_gather(block, axis):
    size = 4
    up = [(i, (i + 1) % size) for i in range(size)]
    down = [(i, (i - 1) % size) for i in range(size)]
    below = lax.ppermute(block, axis, up)
    above = lax.ppermute(block, axis, down)
    half = block.shape[0] // 2
    far_low = lax.ppermute(below[:half], axis, up)
    far_high = lax.ppermute(above[half:], axis, down)
    return [block, below, above, far_low, far_high]


def route(blocks, perms):
    return [blocks[0]] + [lax.ppermute(b, ZRING, p) for b, p in zip(blocks[1:], perms)]


def on_device(queries, query_group, query_bin, query_shift, library, library_bin):
    z_lo = lax.axis_index("rep") // 2
    core = lax.axis_index("rep") % 2
    roles = 4
    slots = roles * CAP

    bin_cols = jnp.pad(library_bin[0].astype(jnp.bfloat16)[:, None], ((0, 0), (0, LANE - 1)))
    partner = lax.ppermute(jnp.concatenate([library[0], bin_cols], axis=1), "blk_1", [(0, 1), (1, 0)])
    own = jnp.concatenate([unit_rows(library[0]), bin_cols], axis=1)
    partner = jnp.concatenate([unit_rows(partner[:, :W]), partner[:, W:]], axis=1)
    half = own.shape[0]
    x_first = ring_gather(own, "blk_0")
    y_first = ring_gather(partner, "blk_2")

    unit_q = unit_rows(queries)
    meta_cols = jnp.stack([query_bin, query_shift], axis=1).astype(jnp.bfloat16)
    unit_q = jnp.concatenate([unit_q, jnp.pad(meta_cols, ((0, 0), (0, LANE - 2)))], axis=1)
    group = query_group[:, 0]
    role = ((group // 2) != z_lo).astype(jnp.int32) * 2 + ((group % 2) != core).astype(jnp.int32)
    slot = slot_index(role, roles, CAP)
    slot_ids = jnp.arange(slots, dtype=jnp.int32)
    placed = slot[:, None] == slot_ids[None, :]
    send_q = lax.dot_general(
        placed.astype(jnp.bfloat16), unit_q, (((0,), (0,)), ((), ())),
        preferred_element_type=jnp.float32,
    ).astype(jnp.bfloat16).reshape(roles, CAP, W + LANE)

    perms = (SIBLING, UP, CROSS)
    received = jnp.concatenate(route([send_q[i] for i in range(roles)], perms), axis=0)
    x_block = jnp.concatenate(x_first, axis=0)
    y_block = jnp.concatenate(y_first, axis=0)
    x_then_y = ring_gather(x_block, "blk_2")
    y_then_x = ring_gather(y_block, "blk_0")
    early = jnp.concatenate([own, partner] + x_first[1:] + y_first[1:], axis=0)
    middle = jnp.concatenate(x_then_y[1:3] + y_then_x[1:3], axis=0)
    late = jnp.concatenate(x_then_y[3:] + y_then_x[3:], axis=0)

    rows = received[:, :W]
    flat_bin = received[:, W].astype(jnp.int32)
    flat_shift = received[:, W + 1].astype(jnp.int32)
    total = rows.shape[0]

    moved = jnp.zeros_like(rows)
    for s in range(1, NSHIFT + 1):
        moved = jnp.where((flat_shift == s)[:, None], lower_bins(rows, s * SHIFT_BINS), moved)
    both = jnp.pad(jnp.concatenate([rows, moved], axis=0), ((0, 0), (0, LANE)))

    def best_of(lib):
        prod = lax.dot_general(lib, both, (((1,), (1,)), ((), ())), preferred_element_type=jnp.float32)
        lib_bins = lib[:, W].astype(jnp.int32)
        near = jnp.abs(lib_bins[:, None] - flat_bin[None, :]) <= WIN
        return top_rows(jnp.where(near, jnp.maximum(prod[:, :total], prod[:, total:]), 0.0))

    best = bitonic_merge(best_of(early), best_of(middle), 1)
    best = bitonic_merge(best, best_of(late), 1)
    best = jnp.concatenate(best, axis=0).T.reshape(roles, CAP, K)

    home = route([best[i] for i in range(roles)], tuple(inverse(p) for p in perms))
    home = jnp.concatenate(home, axis=0)
    return jnp.take(home, slot, axis=0)


def solution(mesh):
    split = Mesh(
        mesh.devices.reshape(4, 2, 4, mesh.shape["rep"]), ("blk_0", "blk_1", "blk_2", "rep")
    )
    in_specs = (
        P(BLK_REP, None),
        P(BLK_REP, None),
        P(BLK_REP),
        P(BLK_REP),
        P("rep", BLK, None),
        P("rep", BLK),
    )
    out_specs = P(BLK_REP, None)
    return jax.shard_map(
        on_device, mesh=split, in_specs=in_specs, out_specs=out_specs, check_vma=False
    )
```

```python
import jax
import jax.numpy as jnp
from jax import lax
from jax.sharding import Mesh
from jax.sharding import PartitionSpec as P

W = 4096
K = 8
NSHIFT = 2
SHIFT_BINS = 16
WIN = 16
CAP = 128
BLK = ("blk_0", "blk_1", "blk_2")
BLK_REP = ("blk_0", "blk_1", "blk_2", "rep")
ZRING = ("blk_1", "rep")


def ring_index(z, core):
    return (z // 2) * 4 + (z % 2) * 2 + core


UP = [(ring_index(z, 0), ring_index((z + 1) % 4, 0)) for z in range(4)] + [
    (ring_index(z, 1), ring_index((z + 3) % 4, 1)) for z in range(4)
]
CROSS = [(ring_index(z, 1), ring_index((z + 1) % 4, 0)) for z in range(4)] + [
    (ring_index(z, 0), ring_index((z + 3) % 4, 1)) for z in range(4)
]
SIBLING = [(ring_index(z, c), ring_index(z, 1 - c)) for z in range(4) for c in range(2)]


def inverse(perm):
    return [(b, a) for a, b in perm]


def unit_rows(raw):
    values = jnp.sqrt(raw.astype(jnp.float32))
    total = jnp.sum(values * values, axis=-1, keepdims=True)
    return (values * lax.rsqrt(total + 1e-06)).astype(jnp.bfloat16)


def lower_bins(rows, amount):
    tail = jnp.zeros(rows.shape[:-1] + (amount,), rows.dtype)
    return jnp.concatenate([rows[..., amount:], tail], axis=-1)


def slot_index(role, roles, capacity):
    labels = jnp.arange(roles, dtype=jnp.int32)
    onehot = (role[:, None] == labels[None, :]).astype(jnp.int32)
    before = jnp.cumsum(onehot, axis=0) - onehot
    place = jnp.sum(before * onehot, axis=1)
    return role * capacity + place


SORT8 = (
    ((0, 1), (2, 3), (4, 5), (6, 7)),
    ((0, 2), (1, 3), (4, 6), (5, 7)),
    ((1, 2), (5, 6)),
    ((0, 4), (1, 5), (2, 6), (3, 7)),
    ((2, 4), (3, 5)),
    ((1, 2), (3, 4), (5, 6)),
)


def exchange(lists, i, j):
    lists[i], lists[j] = jnp.maximum(lists[i], lists[j]), jnp.minimum(lists[i], lists[j])


def top_rows(scores):
    depth = scores.shape[0] // K
    lists = [scores[k * depth:(k + 1) * depth] for k in range(K)]
    for stage in SORT8:
        for i, j in stage:
            exchange(lists, i, j)
    while depth > 1:
        depth //= 2
        lists = [jnp.maximum(lists[i][:depth], lists[K - 1 - i][depth:]) for i in range(K)]
        for step in (4, 2, 1):
            for i in range(K):
                if (i // step) % 2 == 0:
                    exchange(lists, i, i + step)
    return jnp.concatenate(lists, axis=0).T


def route(blocks, perms):
    return [blocks[0]] + [lax.ppermute(b, ZRING, p) for b, p in zip(blocks[1:], perms)]


def on_device(queries, query_group, query_bin, query_shift, library, library_bin):
    lib_rows = library.shape[1]
    z_lo = lax.axis_index("rep") // 2
    core = lax.axis_index("rep") % 2
    roles = 4
    slots = roles * CAP

    partner = lax.ppermute(library[0], "blk_1", [(0, 1), (1, 0)])
    partner_bin = lax.ppermute(library_bin[0], "blk_1", [(0, 1), (1, 0)])
    chunk = jnp.concatenate([unit_rows(library[0]), unit_rows(partner)], axis=0)
    chunk_bin = jnp.concatenate([library_bin[0], partner_bin], axis=0)
    full, lib_bins = lax.all_gather((chunk, chunk_bin), ("blk_0", "blk_2"), axis=0, tiled=True)

    unit_q = unit_rows(queries)
    group = query_group[:, 0]
    role = ((group // 2) != z_lo).astype(jnp.int32) * 2 + ((group % 2) != core).astype(jnp.int32)
    slot = slot_index(role, roles, CAP)
    slot_ids = jnp.arange(slots, dtype=jnp.int32)
    placed = slot[:, None] == slot_ids[None, :]
    placed_int = placed.astype(jnp.int32)
    send_q = lax.dot_general(
        placed.astype(jnp.bfloat16), unit_q, (((0,), (0,)), ((), ())),
        preferred_element_type=jnp.float32,
    ).astype(jnp.bfloat16).reshape(roles, CAP, W)
    send_bin = jnp.sum(placed_int * query_bin[:, None], axis=0).reshape(roles, CAP)
    send_shift = jnp.sum(placed_int * query_shift[:, None], axis=0).reshape(roles, CAP)
    send_meta = jnp.stack([send_bin, send_shift], axis=1)

    perms = (SIBLING, UP, CROSS)
    rows = jnp.concatenate(route([send_q[i] for i in range(roles)], perms), axis=0)
    meta = jnp.stack(route([send_meta[i] for i in range(roles)], perms), axis=0)
    flat_bin = meta[:, 0].reshape(-1)
    flat_shift = meta[:, 1].reshape(-1)
    total = rows.shape[0]

    moved = jnp.zeros_like(rows)
    for s in range(1, NSHIFT + 1):
        moved = jnp.where((flat_shift == s)[:, None], lower_bins(rows, s * SHIFT_BINS), moved)

    def best_for(first, count):
        part = slice(first, first + count)
        both = jnp.concatenate([rows[part], moved[part]], axis=0)
        prod = lax.dot_general(full, both, (((1,), (1,)), ((), ())), preferred_element_type=jnp.float32)
        near = jnp.abs(lib_bins[:, None] - flat_bin[None, part]) <= WIN
        scores = jnp.where(near, jnp.maximum(prod[:, :count], prod[:, count:]), 0.0)
        return top_rows(scores).reshape(count // CAP, CAP, K)

    far = best_for(2 * CAP, 2 * CAP)
    back_up = lax.ppermute(far[0], ZRING, inverse(UP))
    back_cross = lax.ppermute(far[1], ZRING, inverse(CROSS))
    local = best_for(0, 2 * CAP)
    back_sibling = lax.ppermute(local[1], ZRING, inverse(SIBLING))
    home = jnp.concatenate([local[0], back_sibling, back_up, back_cross], axis=0)
    return jnp.take(home, slot, axis=0)


def solution(mesh):
    split = Mesh(
        mesh.devices.reshape(4, 2, 4, mesh.shape["rep"]), ("blk_0", "blk_1", "blk_2", "rep")
    )
    in_specs = (
        P(BLK_REP, None),
        P(BLK_REP, None),
        P(BLK_REP),
        P(BLK_REP),
        P("rep", BLK, None),
        P("rep", BLK),
    )
    out_specs = P(BLK_REP, None)
    return jax.shard_map(
        on_device, mesh=split, in_specs=in_specs, out_specs=out_specs, check_vma=False
    )
```

```python
import jax
import jax.numpy as jnp
from jax import lax
from jax.sharding import Mesh
from jax.sharding import PartitionSpec as P

W = 4096
K = 8
NSHIFT = 2
SHIFT_BINS = 16
WIN = 16
CAP = 128
BLK = ("blk_0", "blk_1", "blk_2")
BLK_REP = ("blk_0", "blk_1", "blk_2", "rep")
ZRING = ("blk_1", "rep")


def ring_index(z, core):
    return (z // 2) * 4 + (z % 2) * 2 + core


UP = [(ring_index(z, 0), ring_index((z + 1) % 4, 0)) for z in range(4)] + [
    (ring_index(z, 1), ring_index((z + 3) % 4, 1)) for z in range(4)
]
CROSS = [(ring_index(z, 1), ring_index((z + 1) % 4, 0)) for z in range(4)] + [
    (ring_index(z, 0), ring_index((z + 3) % 4, 1)) for z in range(4)
]
SIBLING = [(ring_index(z, c), ring_index(z, 1 - c)) for z in range(4) for c in range(2)]


def inverse(perm):
    return [(b, a) for a, b in perm]


def unit_rows(raw):
    values = jnp.sqrt(raw.astype(jnp.float32))
    total = jnp.sum(values * values, axis=-1, keepdims=True)
    return (values * lax.rsqrt(total + 1e-06)).astype(jnp.bfloat16)


def lower_bins(rows, amount):
    tail = jnp.zeros(rows.shape[:-1] + (amount,), rows.dtype)
    return jnp.concatenate([rows[..., amount:], tail], axis=-1)


def slot_index(role, roles, capacity):
    labels = jnp.arange(roles, dtype=jnp.int32)
    onehot = (role[:, None] == labels[None, :]).astype(jnp.int32)
    before = jnp.cumsum(onehot, axis=0) - onehot
    place = jnp.sum(before * onehot, axis=1)
    return role * capacity + place


SORT8 = (
    ((0, 1), (2, 3), (4, 5), (6, 7)),
    ((0, 2), (1, 3), (4, 6), (5, 7)),
    ((1, 2), (5, 6)),
    ((0, 4), (1, 5), (2, 6), (3, 7)),
    ((2, 4), (3, 5)),
    ((1, 2), (3, 4), (5, 6)),
)


def exchange(lists, i, j):
    lists[i], lists[j] = jnp.maximum(lists[i], lists[j]), jnp.minimum(lists[i], lists[j])


def top_rows(scores):
    depth = scores.shape[0] // K
    lists = [scores[k * depth:(k + 1) * depth] for k in range(K)]
    for stage in SORT8:
        for i, j in stage:
            exchange(lists, i, j)
    while depth > 1:
        depth //= 2
        lists = [jnp.maximum(lists[i][:depth], lists[K - 1 - i][depth:]) for i in range(K)]
        for step in (4, 2, 1):
            for i in range(K):
                if (i // step) % 2 == 0:
                    exchange(lists, i, i + step)
    return jnp.concatenate(lists, axis=0)


def route(blocks, perms):
    return [blocks[0]] + [lax.ppermute(b, ZRING, p) for b, p in zip(blocks[1:], perms)]


def on_device(queries, query_group, query_bin, query_shift, library, library_bin):
    lib_rows = library.shape[1]
    z_lo = lax.axis_index("rep") // 2
    core = lax.axis_index("rep") % 2
    roles = 4
    slots = roles * CAP

    partner = lax.ppermute(library[0], "blk_1", [(0, 1), (1, 0)])
    partner_bin = lax.ppermute(library_bin[0], "blk_1", [(0, 1), (1, 0)])
    chunk = jnp.concatenate([unit_rows(library[0]), unit_rows(partner)], axis=0)
    chunk_bin = jnp.concatenate([library_bin[0], partner_bin], axis=0)
    full, lib_bins = lax.all_gather((chunk, chunk_bin), ("blk_0", "blk_2"), axis=0, tiled=True)

    unit_q = unit_rows(queries)
    group = query_group[:, 0]
    role = ((group // 2) != z_lo).astype(jnp.int32) * 2 + ((group % 2) != core).astype(jnp.int32)
    slot = slot_index(role, roles, CAP)
    slot_ids = jnp.arange(slots, dtype=jnp.int32)
    placed = slot[:, None] == slot_ids[None, :]
    placed_int = placed.astype(jnp.int32)
    send_q = lax.dot_general(
        placed.astype(jnp.bfloat16), unit_q, (((0,), (0,)), ((), ())),
        preferred_element_type=jnp.float32,
    ).astype(jnp.bfloat16).reshape(roles, CAP, W)
    send_bin = jnp.sum(placed_int * query_bin[:, None], axis=0).reshape(roles, CAP)
    send_shift = jnp.sum(placed_int * query_shift[:, None], axis=0).reshape(roles, CAP)
    send_meta = jnp.stack([send_bin, send_shift], axis=1)

    perms = (SIBLING, UP, CROSS)
    rows = jnp.concatenate(route([send_q[i] for i in range(roles)], perms), axis=0)
    meta = jnp.stack(route([send_meta[i] for i in range(roles)], perms), axis=0)
    flat_bin = meta[:, 0].reshape(-1)
    flat_shift = meta[:, 1].reshape(-1)
    total = rows.shape[0]

    moved = jnp.zeros_like(rows)
    for s in range(1, NSHIFT + 1):
        moved = jnp.where((flat_shift == s)[:, None], lower_bins(rows, s * SHIFT_BINS), moved)
    both = jnp.concatenate([rows, moved], axis=0)
    prod = lax.dot_general(full, both, (((1,), (1,)), ((), ())), preferred_element_type=jnp.float32)
    near = jnp.abs(lib_bins[:, None] - flat_bin[None, :]) <= WIN
    scores = jnp.where(near, jnp.maximum(prod[:, :total], prod[:, total:]), 0.0)
    best = top_rows(scores)
    home = route([best[:, i * CAP:(i + 1) * CAP] for i in range(roles)], tuple(inverse(p) for p in perms))
    home = jnp.concatenate(home, axis=1)
    return jnp.take(home, slot, axis=1).T


def solution(mesh):
    split = Mesh(
        mesh.devices.reshape(4, 2, 4, mesh.shape["rep"]), ("blk_0", "blk_1", "blk_2", "rep")
    )
    in_specs = (
        P(BLK_REP, None),
        P(BLK_REP, None),
        P(BLK_REP),
        P(BLK_REP),
        P("rep", BLK, None),
        P("rep", BLK),
    )
    out_specs = P(BLK_REP, None)
    return jax.shard_map(
        on_device, mesh=split, in_specs=in_specs, out_specs=out_specs, check_vma=False
    )
```

```python
import jax
import jax.numpy as jnp
from jax import lax
from jax.sharding import Mesh
from jax.sharding import PartitionSpec as P

W = 4096
K = 8
NSHIFT = 2
SHIFT_BINS = 16
WIN = 16
CAP = 128
LANE = 128
BLK = ("blk_0", "blk_1", "blk_2")
BLK_REP = ("blk_0", "blk_1", "blk_2", "rep")
ZRING = ("blk_1", "rep")


def ring_index(z, core):
    return (z // 2) * 4 + (z % 2) * 2 + core


UP = [(ring_index(z, 0), ring_index((z + 1) % 4, 0)) for z in range(4)] + [
    (ring_index(z, 1), ring_index((z + 3) % 4, 1)) for z in range(4)
]
CROSS = [(ring_index(z, 1), ring_index((z + 1) % 4, 0)) for z in range(4)] + [
    (ring_index(z, 0), ring_index((z + 3) % 4, 1)) for z in range(4)
]
SIBLING = [(ring_index(z, c), ring_index(z, 1 - c)) for z in range(4) for c in range(2)]


def inverse(perm):
    return [(b, a) for a, b in perm]


def unit_rows(raw):
    values = jnp.sqrt(raw.astype(jnp.float32))
    total = jnp.sum(values * values, axis=-1, keepdims=True)
    return (values * lax.rsqrt(total + 1e-06)).astype(jnp.bfloat16)


def lower_bins(rows, amount):
    tail = jnp.zeros(rows.shape[:-1] + (amount,), rows.dtype)
    return jnp.concatenate([rows[..., amount:], tail], axis=-1)


def slot_index(role, roles, capacity):
    labels = jnp.arange(roles, dtype=jnp.int32)
    onehot = (role[:, None] == labels[None, :]).astype(jnp.int32)
    before = jnp.cumsum(onehot, axis=0) - onehot
    place = jnp.sum(before * onehot, axis=1)
    return role * capacity + place


SORT8 = (
    ((0, 1), (2, 3), (4, 5), (6, 7)),
    ((0, 2), (1, 3), (4, 6), (5, 7)),
    ((1, 2), (5, 6)),
    ((0, 4), (1, 5), (2, 6), (3, 7)),
    ((2, 4), (3, 5)),
    ((1, 2), (3, 4), (5, 6)),
)


def exchange(lists, i, j):
    lists[i], lists[j] = jnp.maximum(lists[i], lists[j]), jnp.minimum(lists[i], lists[j])


def top_rows(scores):
    depth = scores.shape[0] // K
    assert depth & (depth - 1) == 0
    lists = [scores[k * depth:(k + 1) * depth] for k in range(K)]
    for stage in SORT8:
        for i, j in stage:
            exchange(lists, i, j)
    while depth > 1:
        depth //= 2
        lists = bitonic_merge([a[:depth] for a in lists], [a[depth:] for a in lists])
    return lists


def ring_gather(block, axis):
    size = 4
    up = [(i, (i + 1) % size) for i in range(size)]
    down = [(i, (i - 1) % size) for i in range(size)]
    below = lax.ppermute(block, axis, up)
    above = lax.ppermute(block, axis, down)
    half = block.shape[0] // 2
    far_low = lax.ppermute(below[:half], axis, up)
    far_high = lax.ppermute(above[half:], axis, down)
    return [block, below, above, far_low, far_high]


def bitonic_merge(first, second):
    lists = [jnp.maximum(first[i], second[K - 1 - i]) for i in range(K)]
    for step in (4, 2, 1):
        for i in range(K):
            if (i // step) % 2 == 0:
                exchange(lists, i, i + step)
    return lists


def route(blocks, perms):
    return [blocks[0]] + [lax.ppermute(b, ZRING, p) for b, p in zip(blocks[1:], perms)]


def on_device(queries, query_group, query_bin, query_shift, library, library_bin):
    lib_rows = library.shape[1]
    z_lo = lax.axis_index("rep") // 2
    core = lax.axis_index("rep") % 2
    roles = 4
    slots = roles * CAP

    partner = lax.ppermute(library[0], "blk_1", [(0, 1), (1, 0)])
    partner_bin = lax.ppermute(library_bin[0], "blk_1", [(0, 1), (1, 0)])
    partner = unit_rows(partner)
    kept = 3 * partner.shape[0] // 2 - library.shape[1]
    chunk = jnp.concatenate([unit_rows(library[0]), partner[:kept]], axis=0)
    chunk_bin = jnp.concatenate([library_bin[0], partner_bin[:kept]], axis=0)
    full, lib_bins = lax.all_gather((chunk, chunk_bin), ("blk_0", "blk_2"), axis=0, tiled=True)
    bin_cols = jnp.pad(partner_bin[kept:].astype(jnp.bfloat16)[:, None], ((0, 0), (0, LANE - 1)))
    rest = jnp.concatenate([partner[kept:], bin_cols], axis=1)
    rest = ring_gather(jnp.concatenate(ring_gather(rest, "blk_2"), axis=0), "blk_0")
    rest = jnp.concatenate(rest, axis=0)

    unit_q = unit_rows(queries)
    group = query_group[:, 0]
    role = ((group // 2) != z_lo).astype(jnp.int32) * 2 + ((group % 2) != core).astype(jnp.int32)
    slot = slot_index(role, roles, CAP)
    slot_ids = jnp.arange(slots, dtype=jnp.int32)
    placed = slot[:, None] == slot_ids[None, :]
    placed_int = placed.astype(jnp.int32)
    send_q = lax.dot_general(
        placed.astype(jnp.bfloat16), unit_q, (((0,), (0,)), ((), ())),
        preferred_element_type=jnp.float32,
    ).astype(jnp.bfloat16).reshape(roles, CAP, W)
    send_bin = jnp.sum(placed_int * query_bin[:, None], axis=0).reshape(roles, CAP)
    send_shift = jnp.sum(placed_int * query_shift[:, None], axis=0).reshape(roles, CAP)
    send_meta = jnp.stack([send_bin, send_shift], axis=1)

    perms = (SIBLING, UP, CROSS)
    rows = jnp.concatenate(route([send_q[i] for i in range(roles)], perms), axis=0)
    meta = jnp.stack(route([send_meta[i] for i in range(roles)], perms), axis=0)
    flat_bin = meta[:, 0].reshape(-1)
    flat_shift = meta[:, 1].reshape(-1)
    total = rows.shape[0]

    moved = jnp.zeros_like(rows)
    for s in range(1, NSHIFT + 1):
        moved = jnp.where((flat_shift == s)[:, None], lower_bins(rows, s * SHIFT_BINS), moved)
    both = jnp.concatenate([rows, moved], axis=0)

    def best_of(lib, bins):
        prod = lax.dot_general(lib, both, (((1,), (1,)), ((), ())), preferred_element_type=jnp.float32)
        near = jnp.abs(bins[:, None] - flat_bin[None, :]) <= WIN
        return top_rows(jnp.where(near, jnp.maximum(prod[:, :total], prod[:, total:]), 0.0))

    split_at = full.shape[0] * 2 // 3
    best = best_of(rest[:, :W], rest[:, W].astype(jnp.int32))
    best = bitonic_merge(best, best_of(full[:split_at], lib_bins[:split_at]))
    best = bitonic_merge(best, best_of(full[split_at:], lib_bins[split_at:]))
    best = jnp.concatenate(best, axis=0)

    home = route([best[:, i * CAP:(i + 1) * CAP] for i in range(roles)], tuple(inverse(p) for p in perms))
    home = jnp.concatenate(home, axis=1)
    return jnp.take(home, slot, axis=1).T


def solution(mesh):
    split = Mesh(
        mesh.devices.reshape(4, 2, 4, mesh.shape["rep"]), ("blk_0", "blk_1", "blk_2", "rep")
    )
    in_specs = (
        P(BLK_REP, None),
        P(BLK_REP, None),
        P(BLK_REP),
        P(BLK_REP),
        P("rep", BLK, None),
        P("rep", BLK),
    )
    out_specs = P(BLK_REP, None)
    return jax.shard_map(
        on_device, mesh=split, in_specs=in_specs, out_specs=out_specs, check_vma=False
    )
```

```python
import jax
import jax.numpy as jnp
from jax import lax
from jax.sharding import Mesh
from jax.sharding import PartitionSpec as P

W = 4096
K = 8
NSHIFT = 2
SHIFT_BINS = 16
WIN = 16
CAP = 128
BLK = ("blk_0", "blk_1", "blk_2")
BLK_REP = ("blk_0", "blk_1", "blk_2", "rep")
ZRING = ("blk_1", "rep")


def ring_index(z, core):
    return (z // 2) * 4 + (z % 2) * 2 + core


UP = [(ring_index(z, 0), ring_index((z + 1) % 4, 0)) for z in range(4)] + [
    (ring_index(z, 1), ring_index((z + 3) % 4, 1)) for z in range(4)
]
CROSS = [(ring_index(z, 1), ring_index((z + 1) % 4, 0)) for z in range(4)] + [
    (ring_index(z, 0), ring_index((z + 3) % 4, 1)) for z in range(4)
]
SIBLING = [(ring_index(z, c), ring_index(z, 1 - c)) for z in range(4) for c in range(2)]


def inverse(perm):
    return [(b, a) for a, b in perm]


def unit_rows(raw):
    values = jnp.sqrt(raw.astype(jnp.float32))
    total = jnp.sum(values * values, axis=-1, keepdims=True)
    return (values * lax.rsqrt(total + 1e-06)).astype(jnp.bfloat16)


def lower_bins(rows, amount):
    tail = jnp.zeros(rows.shape[:-1] + (amount,), rows.dtype)
    return jnp.concatenate([rows[..., amount:], tail], axis=-1)


def slot_index(role, roles, capacity):
    labels = jnp.arange(roles, dtype=jnp.int32)
    onehot = (role[:, None] == labels[None, :]).astype(jnp.int32)
    before = jnp.cumsum(onehot, axis=0) - onehot
    place = jnp.sum(before * onehot, axis=1)
    return role * capacity + place


SORT8 = (
    ((0, 1), (2, 3), (4, 5), (6, 7)),
    ((0, 2), (1, 3), (4, 6), (5, 7)),
    ((1, 2), (5, 6)),
    ((0, 4), (1, 5), (2, 6), (3, 7)),
    ((2, 4), (3, 5)),
    ((1, 2), (3, 4), (5, 6)),
)


def exchange(lists, i, j):
    lists[i], lists[j] = jnp.maximum(lists[i], lists[j]), jnp.minimum(lists[i], lists[j])


def top_rows(scores):
    depth = scores.shape[0] // K
    lists = [scores[k * depth:(k + 1) * depth] for k in range(K)]
    for stage in SORT8:
        for i, j in stage:
            exchange(lists, i, j)
    while depth > 1:
        depth //= 2
        lists = [jnp.maximum(lists[i][:depth], lists[K - 1 - i][depth:]) for i in range(K)]
        for step in (4, 2, 1):
            for i in range(K):
                if (i // step) % 2 == 0:
                    exchange(lists, i, i + step)
    return jnp.concatenate(lists, axis=0)


def route(blocks, perms):
    return [blocks[0]] + [lax.ppermute(b, ZRING, p) for b, p in zip(blocks[1:], perms)]


def on_device(queries, query_group, query_bin, query_shift, library, library_bin):
    lib_rows = library.shape[1]
    z_lo = lax.axis_index("rep") // 2
    core = lax.axis_index("rep") % 2
    roles = 4
    slots = roles * CAP

    partner = lax.ppermute(library[0], "blk_1", [(0, 1), (1, 0)])
    partner_bin = lax.ppermute(library_bin[0], "blk_1", [(0, 1), (1, 0)])
    chunk = jnp.concatenate([unit_rows(library[0]), unit_rows(partner)], axis=0)
    chunk_bin = jnp.concatenate([library_bin[0], partner_bin], axis=0)
    full, lib_bins = lax.all_gather((chunk, chunk_bin), ("blk_0", "blk_2"), axis=0, tiled=True)

    unit_q = unit_rows(queries)
    group = query_group[:, 0]
    role = ((group // 2) != z_lo).astype(jnp.int32) * 2 + ((group % 2) != core).astype(jnp.int32)
    slot = slot_index(role, roles, CAP)
    slot_ids = jnp.arange(slots, dtype=jnp.int32)
    placed = slot[:, None] == slot_ids[None, :]
    placed_int = placed.astype(jnp.int32)
    send_q = lax.dot_general(
        placed.astype(jnp.bfloat16), unit_q, (((0,), (0,)), ((), ())),
        preferred_element_type=jnp.float32,
    ).astype(jnp.bfloat16).reshape(roles, CAP, W)
    send_bin = jnp.sum(placed_int * query_bin[:, None], axis=0).reshape(roles, CAP)
    send_shift = jnp.sum(placed_int * query_shift[:, None], axis=0).reshape(roles, CAP)
    send_meta = jnp.stack([send_bin, send_shift], axis=1)

    lib_bins, send_q, send_meta = lax.optimization_barrier((lib_bins, send_q, send_meta))
    perms = (SIBLING, UP, CROSS)
    rows = jnp.concatenate(route([send_q[i] for i in range(roles)], perms), axis=0)
    meta = jnp.stack(route([send_meta[i] for i in range(roles)], perms), axis=0)
    flat_bin = meta[:, 0].reshape(-1)
    flat_shift = meta[:, 1].reshape(-1)
    total = rows.shape[0]

    moved = jnp.zeros_like(rows)
    for s in range(1, NSHIFT + 1):
        moved = jnp.where((flat_shift == s)[:, None], lower_bins(rows, s * SHIFT_BINS), moved)
    both = jnp.concatenate([rows, moved], axis=0)
    prod = lax.dot_general(full, both, (((1,), (1,)), ((), ())), preferred_element_type=jnp.float32)
    near = jnp.abs(lib_bins[:, None] - flat_bin[None, :]) <= WIN
    scores = jnp.where(near, jnp.maximum(prod[:, :total], prod[:, total:]), 0.0)
    best = top_rows(scores)
    home = route([best[:, i * CAP:(i + 1) * CAP] for i in range(roles)], tuple(inverse(p) for p in perms))
    home = jnp.concatenate(home, axis=1)
    return jnp.take(home, slot, axis=1).T


def solution(mesh):
    split = Mesh(
        mesh.devices.reshape(4, 2, 4, mesh.shape["rep"]), ("blk_0", "blk_1", "blk_2", "rep")
    )
    in_specs = (
        P(BLK_REP, None),
        P(BLK_REP, None),
        P(BLK_REP),
        P(BLK_REP),
        P("rep", BLK, None),
        P("rep", BLK),
    )
    out_specs = P(BLK_REP, None)
    return jax.shard_map(
        on_device, mesh=split, in_specs=in_specs, out_specs=out_specs, check_vma=False
    )
```

```python
import jax
import jax.numpy as jnp
from jax import lax
from jax.sharding import Mesh
from jax.sharding import PartitionSpec as P

W = 4096
K = 8
NSHIFT = 2
SHIFT_BINS = 16
WIN = 16
CAP = 128
BLK = ("blk_0", "blk_1", "blk_2")
BLK_REP = ("blk_0", "blk_1", "blk_2", "rep")
ZRING = ("blk_1", "rep")


def ring_index(z, core):
    return (z // 2) * 4 + (z % 2) * 2 + core


UP = [(ring_index(z, 0), ring_index((z + 1) % 4, 0)) for z in range(4)] + [
    (ring_index(z, 1), ring_index((z + 3) % 4, 1)) for z in range(4)
]
CROSS = [(ring_index(z, 1), ring_index((z + 1) % 4, 0)) for z in range(4)] + [
    (ring_index(z, 0), ring_index((z + 3) % 4, 1)) for z in range(4)
]
SIBLING = [(ring_index(z, c), ring_index(z, 1 - c)) for z in range(4) for c in range(2)]


def inverse(perm):
    return [(b, a) for a, b in perm]


def unit_rows(raw):
    values = jnp.sqrt(raw.astype(jnp.float32))
    total = jnp.sum(values * values, axis=-1, keepdims=True)
    return (values * lax.rsqrt(total + 1e-06)).astype(jnp.bfloat16)


def lower_bins(rows, amount):
    tail = jnp.zeros(rows.shape[:-1] + (amount,), rows.dtype)
    return jnp.concatenate([rows[..., amount:], tail], axis=-1)


def slot_index(role, roles, capacity):
    labels = jnp.arange(roles, dtype=jnp.int32)
    onehot = (role[:, None] == labels[None, :]).astype(jnp.int32)
    before = jnp.cumsum(onehot, axis=0) - onehot
    place = jnp.sum(before * onehot, axis=1)
    return role * capacity + place


SORT8 = (
    ((0, 1), (2, 3), (4, 5), (6, 7)),
    ((0, 2), (1, 3), (4, 6), (5, 7)),
    ((1, 2), (5, 6)),
    ((0, 4), (1, 5), (2, 6), (3, 7)),
    ((2, 4), (3, 5)),
    ((1, 2), (3, 4), (5, 6)),
)


def exchange(lists, i, j):
    lists[i], lists[j] = jnp.maximum(lists[i], lists[j]), jnp.minimum(lists[i], lists[j])


def top_rows(scores):
    depth = scores.shape[0] // K
    lists = [scores[k * depth:(k + 1) * depth] for k in range(K)]
    for stage in SORT8:
        for i, j in stage:
            exchange(lists, i, j)
    while depth > 1:
        depth //= 2
        lists = [jnp.maximum(lists[i][:depth], lists[K - 1 - i][depth:]) for i in range(K)]
        for step in (4, 2, 1):
            for i in range(K):
                if (i // step) % 2 == 0:
                    exchange(lists, i, i + step)
    return jnp.concatenate(lists, axis=0)


def route(blocks, perms):
    return [blocks[0]] + [lax.ppermute(b, ZRING, p) for b, p in zip(blocks[1:], perms)]


def on_device(queries, query_group, query_bin, query_shift, library, library_bin):
    lib_rows = library.shape[1]
    z_lo = lax.axis_index("rep") // 2
    core = lax.axis_index("rep") % 2
    roles = 4
    slots = roles * CAP

    partner = lax.ppermute(library[0], "blk_1", [(0, 1), (1, 0)])
    partner_bin = lax.ppermute(library_bin[0], "blk_1", [(0, 1), (1, 0)])
    chunk = jnp.concatenate([unit_rows(library[0]), unit_rows(partner)], axis=0)
    chunk_bin = jnp.concatenate([library_bin[0], partner_bin], axis=0)
    full, lib_bins = lax.all_gather((chunk, chunk_bin), ("blk_0", "blk_2"), axis=0, tiled=True)

    unit_q = unit_rows(queries)
    group = query_group[:, 0]
    role = ((group // 2) != z_lo).astype(jnp.int32) * 2 + ((group % 2) != core).astype(jnp.int32)
    slot = slot_index(role, roles, CAP)
    slot_ids = jnp.arange(slots, dtype=jnp.int32)
    placed = slot[:, None] == slot_ids[None, :]
    placed_int = placed.astype(jnp.int32)
    send_q = lax.dot_general(
        placed.astype(jnp.bfloat16), unit_q, (((0,), (0,)), ((), ())),
        preferred_element_type=jnp.float32,
    ).astype(jnp.bfloat16).reshape(roles, CAP, W)
    send_bin = jnp.sum(placed_int * query_bin[:, None], axis=0).reshape(roles, CAP)
    send_shift = jnp.sum(placed_int * query_shift[:, None], axis=0).reshape(roles, CAP)
    send_meta = jnp.stack([send_bin, send_shift], axis=1)

    perms = (SIBLING, UP, CROSS)
    rows = jnp.concatenate(route([send_q[i] for i in range(roles)], perms), axis=0)
    meta = jnp.stack(route([send_meta[i] for i in range(roles)], perms), axis=0)
    flat_bin = meta[:, 0].reshape(-1)
    flat_shift = meta[:, 1].reshape(-1)
    total = rows.shape[0]

    moved = jnp.zeros_like(rows)
    for s in range(1, NSHIFT + 1):
        moved = jnp.where((flat_shift == s)[:, None], lower_bins(rows, s * SHIFT_BINS), moved)
    both = jnp.concatenate([rows, moved], axis=0)
    prod = lax.dot_general(full, both, (((1,), (1,)), ((), ())), preferred_element_type=jnp.float32)
    near = jnp.abs(lib_bins[:, None] - flat_bin[None, :]) <= WIN
    scores = jnp.where(near, jnp.maximum(prod[:, :total], prod[:, total:]), 0.0)
    best = top_rows(scores)
    home = route([best[:, i * CAP:(i + 1) * CAP] for i in range(roles)], tuple(inverse(p) for p in perms))
    home = jnp.concatenate(home, axis=1)
    return lax.dot_general(
        placed.astype(jnp.float32), home, (((1,), (1,)), ((), ())),
        preferred_element_type=jnp.float32, precision=lax.Precision.HIGHEST,
    )


def solution(mesh):
    split = Mesh(
        mesh.devices.reshape(4, 2, 4, mesh.shape["rep"]), ("blk_0", "blk_1", "blk_2", "rep")
    )
    in_specs = (
        P(BLK_REP, None),
        P(BLK_REP, None),
        P(BLK_REP),
        P(BLK_REP),
        P("rep", BLK, None),
        P("rep", BLK),
    )
    out_specs = P(BLK_REP, None)
    return jax.shard_map(
        on_device, mesh=split, in_specs=in_specs, out_specs=out_specs, check_vma=False
    )
```
